128 devices in a mesh: dp: 8 (over z, core), expert: 16 (over x, y).
Axes of the slice: x: 4, y: 4, z: 4, core: 2. Of those that a mesh axis runs over, the one named last changes fastest.
Arguments:
- tokens: bfloat16 [1024, 6144], P('dp'), may hold values from -6 to 6
- query_weight: bfloat16 [6144, 6144], P(None, 'expert'), may hold values from -1.03593 to 1.03593
- key_value_weight: bfloat16 [6144, 2048], P(None, 'expert'), may hold values from -0.05103104 to 0.05103104
- out_weight: bfloat16 [6144, 6144], P('expert'), may hold values from -0.078125 to 0.078125
- doc_lengths: int32 [8], replicated, may hold values from 1 to 512, 1024 in all
- expert_ids: int32 [1024, 2], P(('dp', 'expert')), may hold values from 0 to 3, all different within a row; in each aligned block of 8 rows (0 to 7, 8 to 15, ...) at most 6 rows name the same one
- router_weight: bfloat16 [6144, 4], replicated, may hold values from -0.078125 to 0.078125
- gate_weight: bfloat16 [6144, 32768], P(None, ('expert', 'dp')), may hold values from -0.078125 to 0.078125
- up_weight: bfloat16 [6144, 32768], P(None, ('expert', 'dp')), may hold values from -0.078125 to 0.078125
- down_weight: bfloat16 [32768, 6144], P(('expert', 'dp')), may hold values from -0.0625 to 0.0625
Outputs:
- layer_out: bfloat16 [1024, 6144], P(('dp', 'expert'))
The draws below stay inside these ranges and needn't reach their ends.
Inputs may be any that keep to these rules, and one draw needn't show every extreme that they name: `expert_ids`: each row names 2 different experts; in each aligned block of 8 rows (the rows of one output block) no expert is named more than 6 times, a bound that some block reaches. `doc_lengths`: positive lengths summing to 1024; the longest is exactly 512.
All inputs are finite; a program needn't handle non-finite values.
Results may differ from the reference program's by a relative error of at most 0.012.
Values may be sent and summed in bfloat16 or wider, within the bound.
No kernel may reach another device: no remote copies, remote signals or barrier semaphores. Data moves between devices by JAX's collectives and lax.ppermute only.
A program may use at most 128 MiB of HBM per device.

```python
import math
import jax
import jax.numpy as jnp
import numpy as np
from jax import lax

D = 6144
HEADS = 48
HD = 128
EXPERTS = 4
HID = 8192
TOP = 2
DOCS = 8
SEQ = 1024
TOKENS = 1024
KVH = 8
QPD = 3
HPK = 6
SLABS = 32
SLAB = 256
ROWS = 8
CAP = 6


def key_columns(key):
    spread = D ** (-0.5)
    key_part = jax.random.truncated_normal(jax.random.fold_in(key, 11), -4.0, 4.0, (D, KVH, HD), jnp.float32) * spread
    value_part = jax.random.truncated_normal(jax.random.fold_in(key, 12), -4.0, 4.0, (D, KVH, HD), jnp.float32) * spread
    return (key_part, value_part)


def draw_key_value_weight(key, part):
    key_part, value_part = key_columns(key)
    return jnp.stack([key_part, value_part], axis=2).reshape(D, 2 * KVH * HD).astype(jnp.bfloat16)


def draw_query_weight(key, part):
    drawn = jax.random.truncated_normal(jax.random.fold_in(key, 13), -4.0, 4.0, (D, HEADS, HD), jnp.float32) * D ** (-0.5)
    return drawn.reshape(D, HEADS * HD).astype(jnp.bfloat16)


def block_levels(rng, shape, cuts, smallest, top_value):
    gain, own = 1.0, jax.random.fold_in(rng, 6)
    for position, blocks in cuts:
        draws = jnp.exp(jax.random.uniform(jax.random.fold_in(own, position), (blocks,), jnp.float32, smallest / len(cuts), top_value / len(cuts)))
        gain = gain * jnp.repeat(draws, shape[position] // blocks).reshape([-1 if axis == position else 1 for axis in range(len(shape))])
    return gain


def profile(number_of, total, most, slope):
    portions = [(1 << 20) // math.isqrt(rank ** slope) + 1 for rank in range(2, number_of + 1)]
    spare, counts = total - most - (number_of - 1), [1] * (number_of - 1)
    while spare > 0:
        free = [i for i in range(number_of - 1) if counts[i] < most]
        pool, budget = sum([portions[i] for i in free]), spare
        for i in free:
            more = min(most - counts[i], max(1, budget * portions[i] // pool), spare)
            counts[i] = counts[i] + more
            spare = spare - more
    return np.array([most] + counts)


def ragged(key, number_of, total, bound, skew):
    if number_of == 2:
        one = jax.random.randint(key, (), max(1, total - bound), min(bound, total - 1) + 1)
        return jnp.stack([one, total - one])
    tallies = jnp.asarray(profile(number_of, total, bound, skew), jnp.int32)
    twos = (number_of - 1) // 2
    source_of, receiver = tallies[1:1 + 2 * twos:2], tallies[2:2 + 2 * twos:2]
    margin = jnp.minimum(source_of - 1, bound - receiver)
    moved = jax.random.randint(jax.random.fold_in(key, 1), (twos,), 0, 1 << 20) % (margin + 1)
    tallies = tallies.at[1:1 + 2 * twos:2].set(source_of - moved).at[2:2 + 2 * twos:2].set(receiver + moved)
    return tallies[jax.random.permutation(jax.random.fold_in(key, 2), number_of)]


def assign_block(own_key, own, number, rows, count, top, reach, skew):
    ranking = jax.random.permutation(own_key, count)
    heavy_load, usual = load_shares(count, rows * top, reach, skew, True), load_shares(count, rows * top, reach, skew, False)
    places = jnp.arange(count)

    def named(lengths, rotation):
        used = int((lengths > 0).sum())
        fixed = max(1, used // 4)
        shifted = fixed + (places - fixed + rotation * (used - fixed)) % max(1, count - fixed)
        return jnp.zeros((count,), jnp.int32).at[ranking[jnp.where(places < fixed, places, shifted)]].set(jnp.asarray(lengths, jnp.int32))

    lengths = jnp.where(number % 4 == 0, named(heavy_load, number // 4), named(usual, number - number // 4 - 1))
    mixed = jax.random.permutation(jax.random.fold_in(own, 3), count)
    giver, sink = mixed[0:count // 2 * 2:2], mixed[1:count // 2 * 2:2]
    slack = jnp.minimum(lengths[giver] - 1, reach - lengths[sink]) // 2
    slack = jnp.where((giver == ranking[0]) | (sink == ranking[0]) | (lengths[sink] == 0), 0, jnp.maximum(slack, 0))
    shifted = jax.random.randint(jax.random.fold_in(own, 4), (count // 2,), 0, 1 << 20) % (slack + 1)
    lengths = lengths.at[giver].add(-shifted).at[sink].add(shifted)
    members = jnp.searchsorted(jnp.cumsum(lengths), jnp.arange(rows * top), side="right").astype(jnp.int32)
    listing = members.reshape(top, rows).T
    listing = listing[jax.random.permutation(jax.random.fold_in(own, 1), rows)]
    rotation = jax.random.randint(jax.random.fold_in(own, 2), (rows, 1), 0, top)
    return jnp.take_along_axis(listing, (jnp.arange(top)[None, :] + rotation) % top, axis=1)


def load_shares(number_of, total, bound, lean, full):
    weights = [(1 << 20) // math.isqrt(rank ** lean) + 1 for rank in range(1, number_of + 1)]
    largest = bound if full else min(bound, max(-(-total // number_of), total * weights[0] // sum(weights)))
    least = 1 if total - largest >= number_of - 1 else 0
    counts, surplus = [largest] + [least] * (number_of - 1), total - largest - least * (number_of - 1)
    while surplus > 0:
        free = [i for i in range(1, number_of) if counts[i] < largest] or [i for i in range(1, number_of) if counts[i] < bound]
        mass, remaining = sum([weights[i] for i in free]), surplus
        for i in free:
            more = min(bound - counts[i], max(1, remaining * weights[i] // mass), surplus)
            counts[i] = counts[i] + more
            surplus = surplus - more
    return np.array(counts)


def gaussian(key, shape, deviation, most, split=(), kind=jnp.bfloat16):
    array = deviation * jax.random.normal(key, shape, jnp.float32)
    if split:
        array = array * block_levels(key, shape, split, -0.22, 0.18)
    return jnp.clip(array, -most, most).astype(kind)


def setup_inputs(seed: int = 0) -> dict:
    splits = jax.random.split(jax.random.key(seed), 11)
    tokens = gaussian(splits[0], (TOKENS, D), 1.0, 6.0, ((0, 8),))
    query_weight = draw_query_weight(jax.random.fold_in(splits[10], 71), 0)
    key_value_weight = draw_key_value_weight(jax.random.fold_in(splits[10], 71), 0)
    out_weight = gaussian(splits[3], (HEADS * HD, D), (HEADS * HD) ** -0.5, 0.078125, ((0, 16),))
    doc_lengths = ragged(splits[4], DOCS, SEQ, SEQ // 2, 2).astype(jnp.int32)
    expert_ids_keys = jax.random.split(jax.random.fold_in(splits[5], 1), TOKENS // ROWS)
    expert_ids_turns = jax.random.permutation(jax.random.fold_in(splits[5], 3), TOKENS // ROWS)
    expert_ids = jax.vmap(lambda own, number: assign_block(jax.random.fold_in(splits[5], 2), own, number, ROWS, EXPERTS, TOP, CAP, 2))(expert_ids_keys, expert_ids_turns).reshape((TOKENS, TOP))
    router_weight = gaussian(splits[6], (D, EXPERTS), D ** -0.5, 0.078125)
    gate_weight = gaussian(splits[7], (D, EXPERTS * HID), D ** -0.5, 0.078125, ((1, 128),))
    up_weight = gaussian(splits[8], (D, EXPERTS * HID), D ** -0.5, 0.078125, ((1, 128),))
    down_weight = gaussian(splits[9], (EXPERTS * HID, D), HID ** -0.5, 0.0625, ((0, 128),))
    return dict(tokens=tokens, query_weight=query_weight, key_value_weight=key_value_weight, out_weight=out_weight, doc_lengths=doc_lengths, expert_ids=expert_ids, router_weight=router_weight, gate_weight=gate_weight, up_weight=up_weight, down_weight=down_weight)


EPSILON = 1e-05
ROPE_BASE = 1000000.0
MASKED_SCORE = -1e+30

def round_half(values):
    return lax.optimization_barrier(values.astype(jnp.bfloat16))

def rms_rows(matrix):
    matrix = matrix.astype(jnp.float32)
    return matrix * lax.rsqrt(lax.optimization_barrier(jnp.mean(matrix * matrix, axis=-1, keepdims=True)) + EPSILON)

def rotate(vectors, positions):
    half_width = vectors.shape[-1] // 2
    frequency = ROPE_BASE ** (-jnp.arange(half_width, dtype=jnp.float32) * 2.0 / vectors.shape[-1])
    angles = positions.astype(jnp.float32)[:, None] * frequency[None, :]
    cosine = jnp.cos(angles)[:, None, :]
    sine_part = jnp.sin(angles)[:, None, :]
    first_half = vectors[..., :half_width]
    second = vectors[..., half_width:]
    return jnp.concatenate([first_half * cosine - second * sine_part, second * cosine + first_half * sine_part], axis=-1)

def doc_layout(doc_lengths, positions):
    doc_ends = jnp.cumsum(doc_lengths).astype(jnp.int32)
    passed = (positions[:, None] >= doc_ends[None, :]).astype(jnp.int32)
    document = lax.optimization_barrier(jnp.sum(passed, axis=1)).astype(jnp.int32)
    doc_start = lax.optimization_barrier(jnp.sum(passed * doc_lengths[None, :], axis=1)).astype(jnp.int32)
    return (document, (positions - doc_start).astype(jnp.int32))

def reference(tokens, query_weight, key_value_weight, out_weight, doc_lengths, expert_ids, router_weight, gate_weight, up_weight, down_weight):
    positions = jnp.arange(TOKENS, dtype=jnp.int32)
    document, in_document = doc_layout(doc_lengths, positions)
    normed_in = rms_rows(tokens).astype(jnp.bfloat16)
    queries = jnp.dot(normed_in, query_weight, preferred_element_type=jnp.float32).reshape(TOKENS, HEADS, HD)
    queries = round_half(rotate(queries, in_document))
    key_value = jnp.dot(normed_in, key_value_weight, preferred_element_type=jnp.float32).reshape(TOKENS, KVH, 2, HD)
    key_rows = round_half(rotate(key_value[:, :, 0, :], in_document))
    values = round_half(key_value[:, :, 1, :])
    allowed = (document[:, None] == document[None, :]) & (positions[None, :] <= positions[:, None])
    block_count = HEADS // QPD

    def one_block(block_index, attention):
        block_index = jnp.asarray(block_index).astype(jnp.int32)
        key_index = (block_index * QPD // HPK).astype(jnp.int32)
        block_query = lax.dynamic_slice_in_dim(queries, block_index * QPD, QPD, 1).astype(jnp.float32)
        block_keys = lax.dynamic_index_in_dim(key_rows, key_index, 1, keepdims=False).astype(jnp.float32)
        block_values = lax.dynamic_index_in_dim(values, key_index, 1, keepdims=False).astype(jnp.float32)
        scores = jnp.einsum('tqd,jd->qtj', block_query, block_keys) * HD ** (-0.5)
        masked = jnp.where(allowed[None], scores, MASKED_SCORE)
        row_max = lax.optimization_barrier(jnp.max(masked, axis=2, keepdims=True))
        expo = jnp.where(allowed[None], jnp.exp(masked - row_max), 0.0)
        denom = lax.optimization_barrier(jnp.sum(expo, axis=2))
        probs = round_half(expo).astype(jnp.float32)
        context = jnp.einsum('qtj,jd->qtd', probs, block_values) / denom[..., None]
        context = jnp.transpose(context, (1, 0, 2)).reshape(TOKENS, QPD * HD).astype(jnp.bfloat16)
        block_out = lax.dynamic_slice_in_dim(out_weight, block_index * (QPD * HD), QPD * HD, 0)
        term = jnp.dot(context, block_out, preferred_element_type=jnp.float32)
        return attention + round_half(term).astype(jnp.float32)
    attention = lax.fori_loop(0, block_count, one_block, jnp.zeros((TOKENS, D), jnp.float32))
    hidden_state = tokens.astype(jnp.float32) + attention
    normed = rms_rows(hidden_state).astype(jnp.bfloat16)
    logits = jnp.dot(normed, router_weight, preferred_element_type=jnp.float32)
    picked = jnp.take_along_axis(logits, expert_ids, axis=1)
    gates = jax.nn.softmax(picked, axis=1)

    def one_expert(moe_sum, expert):
        matches = expert_ids == expert
        weight = lax.optimization_barrier(jnp.sum(jnp.where(matches, gates, 0.0), axis=1))
        chosen = jnp.any(matches, axis=1)
        row_index = jnp.nonzero(chosen, size=TOKENS, fill_value=TOKENS)[0].astype(jnp.int32)
        picked_rows = jnp.take(normed, row_index, axis=0, mode='fill', fill_value=0)
        columns = (expert * HID).astype(jnp.int32)
        expert_gate = lax.dynamic_slice_in_dim(gate_weight, columns, HID, 1)
        expert_up = lax.dynamic_slice_in_dim(up_weight, columns, HID, 1)
        expert_down = lax.dynamic_slice_in_dim(down_weight, columns, HID, 0)
        gate_part = jnp.dot(picked_rows, expert_gate, preferred_element_type=jnp.float32)
        up_part = jnp.dot(picked_rows, expert_up, preferred_element_type=jnp.float32)
        activated = (jax.nn.silu(gate_part) * up_part).astype(jnp.bfloat16)
        produced = jnp.zeros((TOKENS, D), jnp.float32)
        for slab_index in range(SLABS):
            lower = slab_index * SLAB
            term = jnp.dot(activated[:, lower:lower + SLAB], expert_down[lower:lower + SLAB], preferred_element_type=jnp.float32)
            produced = produced + round_half(term).astype(jnp.float32)
        scales = jnp.take(weight, row_index, mode='fill', fill_value=0)
        moe_sum = moe_sum.at[row_index].add(produced * scales[:, None], mode='drop')
        return (moe_sum, None)
    moe, _ = lax.scan(one_expert, jnp.zeros((TOKENS, D), jnp.float32), jnp.arange(EXPERTS, dtype=jnp.int32))
    return (hidden_state + moe).astype(jnp.bfloat16)
```

```python
import jax
import jax.numpy as jnp
import numpy as np
from jax import lax
from jax.sharding import Mesh
from jax.sharding import PartitionSpec as P

HD = 128
CORES = 2

EPSILON = 1e-05
ROPE_BASE = 1000000.0
MASKED_SCORE = -1e30


def rms_rows(matrix):
    matrix = matrix.astype(jnp.float32)
    return matrix * lax.rsqrt(jnp.mean(matrix * matrix, axis=-1, keepdims=True) + EPSILON)


def rotate(vectors, positions):
    half_width = vectors.shape[-1] // 2
    frequency = ROPE_BASE ** (-jnp.arange(half_width, dtype=jnp.float32) * 2.0 / vectors.shape[-1])
    angles = positions.astype(jnp.float32)[:, None] * frequency[None, :]
    cosine = jnp.cos(angles)[:, None, :]
    sine_part = jnp.sin(angles)[:, None, :]
    first_half = vectors[..., :half_width]
    second = vectors[..., half_width:]
    return jnp.concatenate(
        [first_half * cosine - second * sine_part, second * cosine + first_half * sine_part],
        axis=-1,
    )


def doc_layout(doc_lengths, positions):
    doc_ends = jnp.cumsum(doc_lengths)
    passed = (positions[:, None] >= doc_ends[None, :]).astype(jnp.int32)
    document = jnp.sum(passed, axis=1)
    doc_start = jnp.sum(passed * doc_lengths[None, :], axis=1)
    return (document, positions - doc_start)


def per_device(
    tokens,
    query_weight,
    key_value_weight,
    out_weight,
    doc_lengths,
    expert_ids,
    router_weight,
    gate_weight,
    up_weight,
    down_weight,
):
    tok_dev, model_width = tokens.shape
    head_dim = HD
    per_group = query_weight.shape[1] // head_dim
    nx = lax.axis_size("x")
    ny = lax.axis_size("y")
    nc = lax.axis_size("c")
    xi = lax.axis_index("x")
    yi = lax.axis_index("y")
    zi = lax.axis_index("z")
    ci = lax.axis_index("c")
    shard = zi * nc + ci
    group = xi * ny + yi
    experts = router_weight.shape[1]
    own_count = tok_dev // (nx * ny)
    capacity = own_count * 3 // 4

    positions = shard * tok_dev + jnp.arange(tok_dev, dtype=jnp.int32)
    document, in_document = doc_layout(doc_lengths, positions)
    normed_in = rms_rows(tokens).astype(jnp.bfloat16)
    queries = jnp.dot(normed_in, query_weight, preferred_element_type=jnp.float32).reshape(
        tok_dev, per_group, head_dim
    )
    queries = rotate(queries, in_document).astype(jnp.bfloat16)
    half_part = jnp.dot(normed_in, key_value_weight, preferred_element_type=jnp.float32)
    rotated = rotate(half_part[:, None, :], in_document)[:, 0, :]
    holds_keys = group % 2 == 0
    mine = jnp.where(holds_keys, rotated, half_part).astype(jnp.bfloat16)
    pairs = [(i, i ^ 1) for i in range(ny)]
    partner = lax.ppermute(mine, "y", pairs)
    key_rows = jnp.where(holds_keys, mine, partner)
    values = jnp.where(holds_keys, partner, mine)
    both = jnp.stack([key_rows, values], axis=0)
    gathered = lax.all_gather(both, ("z", "c"), axis=1, tiled=True)
    key_piece = gathered[0]
    value_piece = gathered[1]
    piece_rows = key_piece.shape[0]
    key_places = jnp.arange(piece_rows, dtype=jnp.int32)
    key_doc, unused = doc_layout(doc_lengths, key_places)
    allowed = (document[:, None] == key_doc[None, :]) & (key_places[None, :] <= positions[:, None])
    scores = (
        jnp.einsum("tqd,jd->tqj", queries, key_piece, preferred_element_type=jnp.float32)
        * head_dim ** (-0.5)
    )
    masked = jnp.where(allowed[:, None, :], scores, MASKED_SCORE)
    row_max = jnp.max(masked, axis=2)
    expo = jnp.where(allowed[:, None, :], jnp.exp(masked - row_max[..., None]), 0.0)
    denom = jnp.sum(expo, axis=2)
    weighted = jnp.einsum(
        "tqj,jd->tqd", expo.astype(jnp.bfloat16), value_piece, preferred_element_type=jnp.float32
    )
    context = (
        (weighted / denom[..., None]).astype(jnp.bfloat16).reshape(tok_dev, per_group * head_dim)
    )
    partial_value = jnp.dot(context, out_weight, preferred_element_type=jnp.float32)
    attention = lax.psum_scatter(
        partial_value.astype(jnp.bfloat16), ("x", "y"), scatter_dimension=0, tiled=True
    ).astype(jnp.float32)

    own_tokens = lax.dynamic_slice_in_dim(tokens, group * own_count, own_count, 0)
    hidden_state = own_tokens.astype(jnp.float32) + attention
    normed = rms_rows(hidden_state).astype(jnp.bfloat16)
    logits = jnp.dot(normed, router_weight, preferred_element_type=jnp.float32)
    expert_range = jnp.arange(experts, dtype=jnp.int32)
    matches = expert_ids[:, :, None] == expert_range[None, None, :]
    picked = jnp.sum(jnp.where(matches, logits[:, None, :], 0.0), axis=2)
    gates = jax.nn.softmax(picked, axis=1)
    gate_cols = jnp.sum(jnp.where(matches, gates[:, :, None], 0.0), axis=1)
    names = jnp.any(matches, axis=1).astype(jnp.int32)
    slot = jnp.cumsum(names, axis=0) - names
    slot_range = jnp.arange(capacity, dtype=jnp.int32)
    hits = (slot[:, :, None] == slot_range) & (names[:, :, None] > 0)
    send = jnp.einsum(
        "rec,rd->ecd", hits.astype(jnp.bfloat16), normed, preferred_element_type=jnp.float32
    ).astype(jnp.bfloat16)

    arrived = lax.all_to_all(send, "x", split_axis=0, concat_axis=0, tiled=True)
    arrived = arrived.reshape(experts * capacity, model_width)
    rows = lax.all_gather(arrived, ("y", "z"), axis=0, tiled=True)
    rows = lax.all_gather(rows, "c", axis=0, tiled=True)

    gate_part = jnp.dot(rows, gate_weight, preferred_element_type=jnp.float32)
    up_part = jnp.dot(rows, up_weight, preferred_element_type=jnp.float32)
    activated = (jax.nn.silu(gate_part) * up_part).astype(jnp.bfloat16)
    produced = jnp.dot(activated, down_weight, preferred_element_type=jnp.float32).astype(
        jnp.bfloat16
    )

    summed = lax.psum_scatter(produced, "c", scatter_dimension=0, tiled=True)
    summed = lax.psum_scatter(summed, ("y", "z"), scatter_dimension=0, tiled=True)
    summed = summed.reshape(experts, capacity, model_width)
    returned = lax.all_to_all(summed, "x", split_axis=0, concat_axis=0, tiled=True)

    weights = jnp.where(hits, gate_cols[:, :, None], 0.0)
    moe = jnp.einsum(
        "rec,ecd->rd", weights, returned.astype(jnp.float32), precision=lax.Precision.HIGHEST
    )
    return (hidden_state + moe).astype(jnp.bfloat16)


def solution(mesh):
    dp_size = mesh.shape["dp"]

    def run(*args):
        experts = args[6].shape[1]
        ex_size = mesh.shape["expert"]
        devices = np.asarray(mesh.devices).reshape(
            dp_size // CORES, CORES, experts, ex_size // experts
        )
        fine = Mesh(devices, ("z", "c", "x", "y"))
        tok = ("z", "c")
        grp = ("x", "y")
        placed = (
            P(tok, None),
            P(None, grp),
            P(None, grp),
            P(grp, None),
            P(),
            P(tok + grp, None),
            P(),
            P(None, grp + tok),
            P(None, grp + tok),
            P(grp + tok, None),
        )
        body = jax.shard_map(
            per_device, mesh=fine, in_specs=placed, out_specs=P(tok + grp, None), check_vma=False
        )
        return body(*args)

    return run
```

```python
import jax
import jax.numpy as jnp
import numpy as np
from jax import lax
from jax.sharding import Mesh
from jax.sharding import PartitionSpec as P

HD = 128
CORES = 2

EPSILON = 1e-05
ROPE_BASE = 1000000.0
MASKED_SCORE = -1e30


def rms_rows(matrix):
    matrix = matrix.astype(jnp.float32)
    return matrix * lax.rsqrt(jnp.mean(matrix * matrix, axis=-1, keepdims=True) + EPSILON)


def rotate(vectors, positions):
    half_width = vectors.shape[-1] // 2
    frequency = ROPE_BASE ** (-jnp.arange(half_width, dtype=jnp.float32) * 2.0 / vectors.shape[-1])
    angles = positions.astype(jnp.float32)[:, None] * frequency[None, :]
    cosine = jnp.cos(angles)[:, None, :]
    sine_part = jnp.sin(angles)[:, None, :]
    first_half = vectors[..., :half_width]
    second = vectors[..., half_width:]
    return jnp.concatenate(
        [first_half * cosine - second * sine_part, second * cosine + first_half * sine_part],
        axis=-1,
    )


def doc_layout(doc_lengths, positions):
    doc_ends = jnp.cumsum(doc_lengths)
    passed = (positions[:, None] >= doc_ends[None, :]).astype(jnp.int32)
    document = jnp.sum(passed, axis=1)
    doc_start = jnp.sum(passed * doc_lengths[None, :], axis=1)
    return (document, positions - doc_start)


def expert_rows(rows, gate_weight, up_weight, down_weight):
    gate_part = jnp.dot(rows, gate_weight, preferred_element_type=jnp.float32)
    up_part = jnp.dot(rows, up_weight, preferred_element_type=jnp.float32)
    activated = (jax.nn.silu(gate_part) * up_part).astype(jnp.bfloat16)
    return jnp.dot(activated, down_weight, preferred_element_type=jnp.float32).astype(jnp.bfloat16)


def per_device(
    tokens,
    query_weight,
    key_value_weight,
    out_weight,
    doc_lengths,
    expert_ids,
    router_weight,
    gate_weight,
    up_weight,
    down_weight,
):
    tok_dev, model_width = tokens.shape
    head_dim = HD
    per_group = query_weight.shape[1] // head_dim
    nx = lax.axis_size("x")
    ny = lax.axis_size("y")
    nc = lax.axis_size("c")
    xi = lax.axis_index("x")
    yi = lax.axis_index("y")
    zi = lax.axis_index("z")
    ci = lax.axis_index("c")
    shard = zi * nc + ci
    group = xi * ny + yi
    experts = router_weight.shape[1]
    own_count = tok_dev // (nx * ny)
    capacity = own_count * 3 // 4

    positions = shard * tok_dev + jnp.arange(tok_dev, dtype=jnp.int32)
    document, in_document = doc_layout(doc_lengths, positions)
    normed_in = rms_rows(tokens).astype(jnp.bfloat16)
    queries = jnp.dot(normed_in, query_weight, preferred_element_type=jnp.float32).reshape(
        tok_dev, per_group, head_dim
    )
    queries = rotate(queries, in_document).astype(jnp.bfloat16)
    half_part = jnp.dot(normed_in, key_value_weight, preferred_element_type=jnp.float32)
    rotated = rotate(half_part[:, None, :], in_document)[:, 0, :]
    holds_keys = group % 2 == 0
    mine = jnp.where(holds_keys, rotated, half_part).astype(jnp.bfloat16)
    pairs = [(i, i ^ 1) for i in range(ny)]
    partner = lax.ppermute(mine, "y", pairs)
    key_rows = jnp.where(holds_keys, mine, partner)
    values = jnp.where(holds_keys, partner, mine)
    both = jnp.stack([key_rows, values], axis=0)
    gathered = lax.all_gather(both, ("z", "c"), axis=1, tiled=True)
    key_piece = gathered[0]
    value_piece = gathered[1]
    piece_rows = key_piece.shape[0]
    key_places = jnp.arange(piece_rows, dtype=jnp.int32)
    key_doc, unused = doc_layout(doc_lengths, key_places)
    allowed = (document[:, None] == key_doc[None, :]) & (key_places[None, :] <= positions[:, None])
    scores = (
        jnp.einsum("tqd,jd->tqj", queries, key_piece, preferred_element_type=jnp.float32)
        * head_dim ** (-0.5)
    )
    masked = jnp.where(allowed[:, None, :], scores, MASKED_SCORE)
    row_max = jnp.max(masked, axis=2)
    expo = jnp.where(allowed[:, None, :], jnp.exp(masked - row_max[..., None]), 0.0)
    denom = jnp.sum(expo, axis=2)
    weighted = jnp.einsum(
        "tqj,jd->tqd", expo.astype(jnp.bfloat16), value_piece, preferred_element_type=jnp.float32
    )
    context = (
        (weighted / denom[..., None]).astype(jnp.bfloat16).reshape(tok_dev, per_group * head_dim)
    )
    partial_value = jnp.dot(context, out_weight, preferred_element_type=jnp.float32)
    blocks = partial_value.astype(jnp.bfloat16).reshape(nx * ny, own_count, model_width)
    attention = jnp.sum(
        lax.all_to_all(blocks, ("x", "y"), split_axis=0, concat_axis=0, tiled=True).astype(
            jnp.float32
        ),
        axis=0,
    )

    own_tokens = lax.dynamic_slice_in_dim(tokens, group * own_count, own_count, 0)
    hidden_state = own_tokens.astype(jnp.float32) + attention
    normed = rms_rows(hidden_state).astype(jnp.bfloat16)
    logits = jnp.dot(normed, router_weight, preferred_element_type=jnp.float32)
    expert_range = jnp.arange(experts, dtype=jnp.int32)
    matches = expert_ids[:, :, None] == expert_range[None, None, :]
    picked = jnp.sum(jnp.where(matches, logits[:, None, :], 0.0), axis=2)
    gates = jax.nn.softmax(picked, axis=1)
    gate_cols = jnp.sum(jnp.where(matches, gates[:, :, None], 0.0), axis=1)
    names = jnp.any(matches, axis=1).astype(jnp.int32)
    slot = jnp.cumsum(names, axis=0) - names
    slot_range = jnp.arange(capacity, dtype=jnp.int32)
    hits = (slot[:, :, None] == slot_range) & (names[:, :, None] > 0)
    send = jnp.einsum(
        "rec,rd->ecd", hits.astype(jnp.bfloat16), normed, preferred_element_type=jnp.float32
    ).astype(jnp.bfloat16)

    arrived = lax.all_to_all(send, "x", split_axis=0, concat_axis=0, tiled=True)
    arrived = arrived.reshape(experts * capacity, model_width)
    rows = lax.all_gather(arrived, ("y", "z"), axis=0, tiled=True)
    core_swap = [(i, i ^ 1) for i in range(nc)]
    other_rows = lax.ppermute(rows, "c", core_swap)
    own_out = expert_rows(rows, gate_weight, up_weight, down_weight)
    other_out = expert_rows(other_rows, gate_weight, up_weight, down_weight)
    other_back = lax.ppermute(other_out, "c", core_swap)
    summed = (own_out.astype(jnp.float32) + other_back.astype(jnp.float32)).astype(jnp.bfloat16)

    lines = summed.reshape(-1, experts * capacity, model_width)
    summed = jnp.sum(
        lax.all_to_all(lines, ("y", "z"), split_axis=0, concat_axis=0, tiled=True).astype(
            jnp.float32
        ),
        axis=0,
    )
    summed = summed.reshape(experts, capacity, model_width)
    returned = lax.all_to_all(summed, "x", split_axis=0, concat_axis=0, tiled=True)

    weights = jnp.where(hits, gate_cols[:, :, None], 0.0)
    moe = jnp.einsum(
        "rec,ecd->rd", weights, returned, precision=lax.Precision.HIGHEST
    )
    return (hidden_state + moe).astype(jnp.bfloat16)


def solution(mesh):
    dp_size = mesh.shape["dp"]

    def run(*args):
        experts = args[6].shape[1]
        ex_size = mesh.shape["expert"]
        devices = np.asarray(mesh.devices).reshape(
            dp_size // CORES, CORES, experts, ex_size // experts
        )
        fine = Mesh(devices, ("z", "c", "x", "y"))
        tok = ("z", "c")
        grp = ("x", "y")
        placed = (
            P(tok, None),
            P(None, grp),
            P(None, grp),
            P(grp, None),
            P(),
            P(tok + grp, None),
            P(),
            P(None, grp + tok),
            P(None, grp + tok),
            P(grp + tok, None),
        )
        body = jax.shard_map(
            per_device, mesh=fine, in_specs=placed, out_specs=P(tok + grp, None), check_vma=False
        )
        return body(*args)

    return run
```

```python
import jax
import jax.numpy as jnp
import numpy as np
from jax import lax
from jax.sharding import Mesh
from jax.sharding import PartitionSpec as P


HD = 128
CORES = 2
CHUNKS = 2

EPSILON = 1e-05
ROPE_BASE = 1000000.0
MASKED_SCORE = -1e30


def rms_rows(matrix):
    matrix = matrix.astype(jnp.float32)
    return matrix * lax.rsqrt(jnp.mean(matrix * matrix, axis=-1, keepdims=True) + EPSILON)


def rotate(vectors, positions):
    half_width = vectors.shape[-1] // 2
    frequency = ROPE_BASE ** (-jnp.arange(half_width, dtype=jnp.float32) * 2.0 / vectors.shape[-1])
    angles = positions.astype(jnp.float32)[:, None] * frequency[None, :]
    cosine = jnp.cos(angles)[:, None, :]
    sine_part = jnp.sin(angles)[:, None, :]
    first_half = vectors[..., :half_width]
    second = vectors[..., half_width:]
    return jnp.concatenate(
        [first_half * cosine - second * sine_part, second * cosine + first_half * sine_part],
        axis=-1,
    )


def doc_layout(doc_lengths, positions):
    doc_ends = jnp.cumsum(doc_lengths)
    passed = (positions[:, None] >= doc_ends[None, :]).astype(jnp.int32)
    document = jnp.sum(passed, axis=1)
    doc_start = jnp.sum(passed * doc_lengths[None, :], axis=1)
    return (document, positions - doc_start)


def expert_rows(rows, gate_weight, up_weight, down_weight):
    gate_part = jnp.dot(rows, gate_weight, preferred_element_type=jnp.float32)
    up_part = jnp.dot(rows, up_weight, preferred_element_type=jnp.float32)
    activated = (jax.nn.silu(gate_part) * up_part).astype(jnp.bfloat16)
    return jnp.dot(activated, down_weight, preferred_element_type=jnp.float32).astype(jnp.bfloat16)


def per_device(
    tokens,
    query_weight,
    key_value_weight,
    out_weight,
    doc_lengths,
    expert_ids,
    router_weight,
    gate_weight,
    up_weight,
    down_weight,
):
    tok_dev, model_width = tokens.shape
    head_dim = HD
    per_group = query_weight.shape[1] // head_dim
    nx = lax.axis_size("x")
    ny = lax.axis_size("y")
    nc = lax.axis_size("c")
    xi = lax.axis_index("x")
    yi = lax.axis_index("y")
    zi = lax.axis_index("z")
    ci = lax.axis_index("c")
    shard = zi * nc + ci
    group = xi * ny + yi
    experts = router_weight.shape[1]
    own_count = tok_dev // (nx * ny)
    capacity = own_count * 3 // 4

    positions = shard * tok_dev + jnp.arange(tok_dev, dtype=jnp.int32)
    document, in_document = doc_layout(doc_lengths, positions)
    normed_in = rms_rows(tokens).astype(jnp.bfloat16)
    queries = jnp.dot(normed_in, query_weight, preferred_element_type=jnp.float32).reshape(
        tok_dev, per_group, head_dim
    )
    queries = rotate(queries, in_document).astype(jnp.bfloat16)
    half_part = jnp.dot(normed_in, key_value_weight, preferred_element_type=jnp.float32)
    rotated = rotate(half_part[:, None, :], in_document)[:, 0, :]
    holds_keys = group % 2 == 0
    mine = jnp.where(holds_keys, rotated, half_part).astype(jnp.bfloat16)
    pairs = [(i, i ^ 1) for i in range(ny)]
    partner = lax.ppermute(mine, "y", pairs)
    key_rows = jnp.where(holds_keys, mine, partner)
    values = jnp.where(holds_keys, partner, mine)
    both = jnp.stack([key_rows, values], axis=0)
    gathered = lax.all_gather(both, ("z", "c"), axis=1, tiled=True)
    key_piece = gathered[0]
    value_piece = gathered[1]
    piece_rows = key_piece.shape[0]
    key_places = jnp.arange(piece_rows, dtype=jnp.int32)
    key_doc, _ = doc_layout(doc_lengths, key_places)
    allowed = (document[:, None] == key_doc[None, :]) & (key_places[None, :] <= positions[:, None])
    scores = (
        jnp.einsum("tqd,jd->tqj", queries, key_piece, preferred_element_type=jnp.float32)
        * head_dim ** (-0.5)
    )
    masked = jnp.where(allowed[:, None, :], scores, MASKED_SCORE)
    row_max = jnp.max(masked, axis=2)
    expo = jnp.where(allowed[:, None, :], jnp.exp(masked - row_max[..., None]), 0.0)
    denom = jnp.sum(expo, axis=2)
    weighted = jnp.einsum(
        "tqj,jd->tqd", expo.astype(jnp.bfloat16), value_piece, preferred_element_type=jnp.float32
    )
    context = (
        (weighted / denom[..., None]).astype(jnp.bfloat16).reshape(tok_dev, per_group * head_dim)
    )
    partial_value = jnp.dot(context, out_weight, preferred_element_type=jnp.float32)
    blocks = partial_value.astype(jnp.bfloat16).reshape(nx * ny, own_count, model_width)
    attention = jnp.sum(
        lax.all_to_all(blocks, ("x", "y"), split_axis=0, concat_axis=0, tiled=True).astype(
            jnp.float32
        ),
        axis=0,
    )

    own_tokens = lax.dynamic_slice_in_dim(tokens, group * own_count, own_count, 0)
    hidden_state = own_tokens.astype(jnp.float32) + attention
    normed = rms_rows(hidden_state).astype(jnp.bfloat16)
    logits = jnp.dot(normed, router_weight, preferred_element_type=jnp.float32)
    expert_range = jnp.arange(experts, dtype=jnp.int32)
    matches = expert_ids[:, :, None] == expert_range[None, None, :]
    picked = jnp.sum(jnp.where(matches, logits[:, None, :], 0.0), axis=2)
    gates = jax.nn.softmax(picked, axis=1)
    gate_cols = jnp.sum(jnp.where(matches, gates[:, :, None], 0.0), axis=1)
    names = jnp.any(matches, axis=1).astype(jnp.int32)
    slot = jnp.cumsum(names, axis=0) - names
    slot_range = jnp.arange(capacity, dtype=jnp.int32)
    hits = (slot[:, :, None] == slot_range) & (names[:, :, None] > 0)
    send = jnp.einsum(
        "rec,rd->ecd", hits.astype(jnp.bfloat16), normed, preferred_element_type=jnp.float32
    ).astype(jnp.bfloat16)

    arrived = lax.all_to_all(send, "x", split_axis=0, concat_axis=0, tiled=True)
    arrived = arrived.reshape(experts * capacity, model_width)
    core_swap = [(i, i ^ 1) for i in range(nc)]
    chunk_rows = experts * capacity // CHUNKS
    results = []
    for part in range(CHUNKS):
        piece = arrived[part * chunk_rows:(part + 1) * chunk_rows]
        rows = lax.all_gather(piece, ("y", "z"), axis=0, tiled=True)
        other_rows = lax.ppermute(rows, "c", core_swap)
        own_out = expert_rows(rows, gate_weight, up_weight, down_weight)
        other_out = expert_rows(other_rows, gate_weight, up_weight, down_weight)
        other_back = lax.ppermute(other_out, "c", core_swap)
        summed = (own_out.astype(jnp.float32) + other_back.astype(jnp.float32)).astype(jnp.bfloat16)
        lines = summed.reshape(-1, chunk_rows, model_width)
        spread = lax.all_to_all(lines, ("y", "z"), split_axis=0, concat_axis=0, tiled=True)
        results.append(jnp.sum(spread.astype(jnp.float32), axis=0))
    summed = jnp.concatenate(results, axis=0)
    summed = summed.reshape(experts, capacity, model_width)
    returned = lax.all_to_all(summed, "x", split_axis=0, concat_axis=0, tiled=True)

    weights = jnp.where(hits, gate_cols[:, :, None], 0.0)
    moe = jnp.einsum(
        "rec,ecd->rd", weights, returned, precision=lax.Precision.HIGHEST
    )
    return (hidden_state + moe).astype(jnp.bfloat16)


def solution(mesh):
    dp_size = mesh.shape["dp"]

    def run(*args):
        experts = args[6].shape[1]
        ex_size = mesh.shape["expert"]
        devices = np.asarray(mesh.devices).reshape(
            dp_size // CORES, CORES, experts, ex_size // experts
        )
        fine = Mesh(devices, ("z", "c", "x", "y"))
        tok = ("z", "c")
        grp = ("x", "y")
        placed = (
            P(tok, None),
            P(None, grp),
            P(None, grp),
            P(grp, None),
            P(),
            P(tok + grp, None),
            P(),
            P(None, grp + tok),
            P(None, grp + tok),
            P(grp + tok, None),
        )
        body = jax.shard_map(
            per_device, mesh=fine, in_specs=placed, out_specs=P(tok + grp, None), check_vma=False
        )
        return body(*args)

    return run
```

```python
import jax
import jax.numpy as jnp
import numpy as np
from jax import lax
from jax.sharding import Mesh
from jax.sharding import PartitionSpec as P

HD = 128
CORES = 2

EPSILON = 1e-05
ROPE_BASE = 1000000.0
MASKED_SCORE = -1e30


def rms_rows(matrix):
    matrix = matrix.astype(jnp.float32)
    return matrix * lax.rsqrt(jnp.mean(matrix * matrix, axis=-1, keepdims=True) + EPSILON)


def rotate(vectors, positions):
    half_width = vectors.shape[-1] // 2
    frequency = ROPE_BASE ** (-jnp.arange(half_width, dtype=jnp.float32) * 2.0 / vectors.shape[-1])
    angles = positions.astype(jnp.float32)[:, None] * frequency[None, :]
    cosine = jnp.cos(angles)[:, None, :]
    sine_part = jnp.sin(angles)[:, None, :]
    first_half = vectors[..., :half_width]
    second = vectors[..., half_width:]
    return jnp.concatenate(
        [first_half * cosine - second * sine_part, second * cosine + first_half * sine_part],
        axis=-1,
    )


def doc_layout(doc_lengths, positions):
    doc_ends = jnp.cumsum(doc_lengths)
    passed = (positions[:, None] >= doc_ends[None, :]).astype(jnp.int32)
    document = jnp.sum(passed, axis=1)
    doc_start = jnp.sum(passed * doc_lengths[None, :], axis=1)
    return (document, positions - doc_start)


def expert_rows(rows, gate_weight, up_weight, down_weight):
    gate_part = jnp.dot(rows, gate_weight, preferred_element_type=jnp.float32)
    up_part = jnp.dot(rows, up_weight, preferred_element_type=jnp.float32)
    activated = (jax.nn.silu(gate_part) * up_part).astype(jnp.bfloat16)
    return jnp.dot(activated, down_weight, preferred_element_type=jnp.float32).astype(jnp.bfloat16)


def per_device(
    tokens,
    query_weight,
    key_value_weight,
    out_weight,
    doc_lengths,
    expert_ids,
    router_weight,
    gate_weight,
    up_weight,
    down_weight,
):
    tok_dev, model_width = tokens.shape
    head_dim = HD
    per_group = query_weight.shape[1] // head_dim
    nx = lax.axis_size("x")
    ny = lax.axis_size("y")
    nc = lax.axis_size("c")
    xi = lax.axis_index("x")
    yi = lax.axis_index("y")
    zi = lax.axis_index("z")
    ci = lax.axis_index("c")
    shard = zi * nc + ci
    group = xi * ny + yi
    experts = router_weight.shape[1]
    own_count = tok_dev // (nx * ny)
    capacity = own_count * 3 // 4

    positions = shard * tok_dev + jnp.arange(tok_dev, dtype=jnp.int32)
    document, in_document = doc_layout(doc_lengths, positions)
    normed_in = rms_rows(tokens).astype(jnp.bfloat16)
    queries = jnp.dot(normed_in, query_weight, preferred_element_type=jnp.float32).reshape(
        tok_dev, per_group, head_dim
    )
    queries = rotate(queries, in_document).astype(jnp.bfloat16)
    half_part = jnp.dot(normed_in, key_value_weight, preferred_element_type=jnp.float32)
    rotated = rotate(half_part[:, None, :], in_document)[:, 0, :]
    holds_keys = group % 2 == 0
    mine = jnp.where(holds_keys, rotated, half_part).astype(jnp.bfloat16)
    pairs = [(i, i ^ 1) for i in range(ny)]
    partner = lax.ppermute(mine, "y", pairs)
    key_rows = jnp.where(holds_keys, mine, partner)
    values = jnp.where(holds_keys, partner, mine)
    both = jnp.stack([key_rows, values], axis=0)
    gathered = lax.all_gather(both, ("z", "c"), axis=1, tiled=True)
    key_piece = gathered[0]
    value_piece = gathered[1]
    piece_rows = key_piece.shape[0]
    key_places = jnp.arange(piece_rows, dtype=jnp.int32)
    key_doc, unused = doc_layout(doc_lengths, key_places)
    allowed = (document[:, None] == key_doc[None, :]) & (key_places[None, :] <= positions[:, None])
    scores = (
        jnp.einsum("tqd,jd->tqj", queries, key_piece, preferred_element_type=jnp.float32)
        * head_dim ** (-0.5)
    )
    masked = jnp.where(allowed[:, None, :], scores, MASKED_SCORE)
    row_max = jnp.max(masked, axis=2)
    expo = jnp.where(allowed[:, None, :], jnp.exp(masked - row_max[..., None]), 0.0)
    denom = jnp.sum(expo, axis=2)
    weighted = jnp.einsum(
        "tqj,jd->tqd", expo.astype(jnp.bfloat16), value_piece, preferred_element_type=jnp.float32
    )
    context = (
        (weighted / denom[..., None]).astype(jnp.bfloat16).reshape(tok_dev, per_group * head_dim)
    )
    partial_value = jnp.dot(context, out_weight, preferred_element_type=jnp.float32)
    blocks = partial_value.astype(jnp.bfloat16).reshape(nx * ny, own_count, model_width)
    attention = jnp.sum(
        lax.all_to_all(blocks, ("x", "y"), split_axis=0, concat_axis=0, tiled=True).astype(
            jnp.float32
        ),
        axis=0,
    )

    own_tokens = lax.dynamic_slice_in_dim(tokens, group * own_count, own_count, 0)
    hidden_state = own_tokens.astype(jnp.float32) + attention
    normed = rms_rows(hidden_state).astype(jnp.bfloat16)
    logits = jnp.dot(normed, router_weight, preferred_element_type=jnp.float32)
    expert_range = jnp.arange(experts, dtype=jnp.int32)
    matches = expert_ids[:, :, None] == expert_range[None, None, :]
    picked = jnp.sum(jnp.where(matches, logits[:, None, :], 0.0), axis=2)
    gates = jax.nn.softmax(picked, axis=1)
    gate_cols = jnp.sum(jnp.where(matches, gates[:, :, None], 0.0), axis=1)
    names = jnp.any(matches, axis=1).astype(jnp.int32)
    slot = jnp.cumsum(names, axis=0) - names
    slot_range = jnp.arange(capacity, dtype=jnp.int32)
    hits = (slot[:, :, None] == slot_range) & (names[:, :, None] > 0)
    send = jnp.einsum(
        "rec,rd->ecd", hits.astype(jnp.bfloat16), normed, preferred_element_type=jnp.float32
    ).astype(jnp.bfloat16)

    arrived = lax.all_to_all(send, "x", split_axis=0, concat_axis=0, tiled=True)
    arrived = arrived.reshape(experts * capacity, model_width)
    rows = lax.all_gather(arrived, ("c", "y", "z"), axis=0, tiled=True)
    line_rows = rows.shape[0] // nc
    other_rows = lax.dynamic_slice_in_dim(rows, (1 - ci) * line_rows, line_rows, 0)
    own_rows = lax.dynamic_slice_in_dim(rows, ci * line_rows, line_rows, 0)
    core_swap = [(i, i ^ 1) for i in range(nc)]
    other_out = expert_rows(other_rows, gate_weight, up_weight, down_weight)
    other_back = lax.ppermute(other_out, "c", core_swap)
    own_out = expert_rows(own_rows, gate_weight, up_weight, down_weight)
    summed = (own_out.astype(jnp.float32) + other_back.astype(jnp.float32)).astype(jnp.bfloat16)

    lines = summed.reshape(-1, experts * capacity, model_width)
    summed = jnp.sum(
        lax.all_to_all(lines, ("y", "z"), split_axis=0, concat_axis=0, tiled=True).astype(
            jnp.float32
        ),
        axis=0,
    )
    summed = summed.reshape(experts, capacity, model_width)
    returned = lax.all_to_all(summed, "x", split_axis=0, concat_axis=0, tiled=True)

    weights = jnp.where(hits, gate_cols[:, :, None], 0.0)
    moe = jnp.einsum(
        "rec,ecd->rd", weights, returned, precision=lax.Precision.HIGHEST
    )
    return (hidden_state + moe).astype(jnp.bfloat16)


def solution(mesh):
    dp_size = mesh.shape["dp"]

    def run(*args):
        experts = args[6].shape[1]
        ex_size = mesh.shape["expert"]
        devices = np.asarray(mesh.devices).reshape(
            dp_size // CORES, CORES, experts, ex_size // experts
        )
        fine = Mesh(devices, ("z", "c", "x", "y"))
        tok = ("z", "c")
        grp = ("x", "y")
        placed = (
            P(tok, None),
            P(None, grp),
            P(None, grp),
            P(grp, None),
            P(),
            P(tok + grp, None),
            P(),
            P(None, grp + tok),
            P(None, grp + tok),
            P(grp + tok, None),
        )
        body = jax.shard_map(
            per_device, mesh=fine, in_specs=placed, out_specs=P(tok + grp, None), check_vma=False
        )
        return body(*args)

    return run
```

```python
import jax
import jax.numpy as jnp
import numpy as np
from jax import lax
from jax.sharding import Mesh
from jax.sharding import PartitionSpec as P

HD = 128
CORES = 2

EPSILON = 1e-05
ROPE_BASE = 1000000.0
MASKED_SCORE = -1e30


def rms_rows(matrix):
    matrix = matrix.astype(jnp.float32)
    return matrix * lax.rsqrt(jnp.mean(matrix * matrix, axis=-1, keepdims=True) + EPSILON)


def rotate(vectors, positions):
    half_width = vectors.shape[-1] // 2
    frequency = ROPE_BASE ** (-jnp.arange(half_width, dtype=jnp.float32) * 2.0 / vectors.shape[-1])
    angles = positions.astype(jnp.float32)[:, None] * frequency[None, :]
    cosine = jnp.cos(angles)[:, None, :]
    sine_part = jnp.sin(angles)[:, None, :]
    first_half = vectors[..., :half_width]
    second = vectors[..., half_width:]
    return jnp.concatenate(
        [first_half * cosine - second * sine_part, second * cosine + first_half * sine_part],
        axis=-1,
    )


def doc_layout(doc_lengths, positions):
    doc_ends = jnp.cumsum(doc_lengths)
    passed = (positions[:, None] >= doc_ends[None, :]).astype(jnp.int32)
    document = jnp.sum(passed, axis=1)
    doc_start = jnp.sum(passed * doc_lengths[None, :], axis=1)
    return (document, positions - doc_start)


def expert_rows(rows, gate_weight, up_weight, down_weight):
    gate_part = jnp.dot(rows, gate_weight, preferred_element_type=jnp.float32)
    up_part = jnp.dot(rows, up_weight, preferred_element_type=jnp.float32)
    activated = lax.optimization_barrier((jax.nn.silu(gate_part) * up_part).astype(jnp.bfloat16))
    return jnp.dot(activated, down_weight, preferred_element_type=jnp.float32).astype(jnp.bfloat16)


def per_device(
    tokens,
    query_weight,
    key_value_weight,
    out_weight,
    doc_lengths,
    expert_ids,
    router_weight,
    gate_weight,
    up_weight,
    down_weight,
):
    tok_dev, model_width = tokens.shape
    head_dim = HD
    per_group = query_weight.shape[1] // head_dim
    nx = lax.axis_size("x")
    ny = lax.axis_size("y")
    nc = lax.axis_size("c")
    xi = lax.axis_index("x")
    yi = lax.axis_index("y")
    zi = lax.axis_index("z")
    ci = lax.axis_index("c")
    shard = zi * nc + ci
    group = xi * ny + yi
    experts = router_weight.shape[1]
    own_count = tok_dev // (nx * ny)
    capacity = own_count * 3 // 4

    positions = shard * tok_dev + jnp.arange(tok_dev, dtype=jnp.int32)
    document, in_document = doc_layout(doc_lengths, positions)
    normed_in = rms_rows(tokens).astype(jnp.bfloat16)
    queries = jnp.dot(normed_in, query_weight, preferred_element_type=jnp.float32).reshape(
        tok_dev, per_group, head_dim
    )
    queries = rotate(queries, in_document).astype(jnp.bfloat16)
    half_part = jnp.dot(normed_in, key_value_weight, preferred_element_type=jnp.float32)
    rotated = rotate(half_part[:, None, :], in_document)[:, 0, :]
    holds_keys = group % 2 == 0
    mine = jnp.where(holds_keys, rotated, half_part).astype(jnp.bfloat16)
    pairs = [(i, i ^ 1) for i in range(ny)]
    partner = lax.ppermute(mine, "y", pairs)
    key_rows = jnp.where(holds_keys, mine, partner)
    values = jnp.where(holds_keys, partner, mine)
    both = jnp.stack([key_rows, values], axis=0)
    gathered = lax.all_gather(both, ("z", "c"), axis=1, tiled=True)
    key_piece = gathered[0]
    value_piece = gathered[1]
    piece_rows = key_piece.shape[0]
    key_places = jnp.arange(piece_rows, dtype=jnp.int32)
    key_doc, unused = doc_layout(doc_lengths, key_places)
    allowed = (document[:, None] == key_doc[None, :]) & (key_places[None, :] <= positions[:, None])
    scores = (
        jnp.einsum("tqd,jd->tqj", queries, key_piece, preferred_element_type=jnp.float32)
        * head_dim ** (-0.5)
    )
    masked = jnp.where(allowed[:, None, :], scores, MASKED_SCORE)
    row_max = jnp.max(masked, axis=2)
    expo = jnp.where(allowed[:, None, :], jnp.exp(masked - row_max[..., None]), 0.0)
    denom = jnp.sum(expo, axis=2)
    weighted = jnp.einsum(
        "tqj,jd->tqd", expo.astype(jnp.bfloat16), value_piece, preferred_element_type=jnp.float32
    )
    context = (
        (weighted / denom[..., None]).astype(jnp.bfloat16).reshape(tok_dev, per_group * head_dim)
    )
    partial_value = jnp.dot(context, out_weight, preferred_element_type=jnp.float32)
    blocks = partial_value.astype(jnp.bfloat16).reshape(nx * ny, own_count, model_width)
    attention = jnp.sum(
        lax.all_to_all(blocks, ("x", "y"), split_axis=0, concat_axis=0, tiled=True).astype(
            jnp.float32
        ),
        axis=0,
    )

    own_tokens = lax.dynamic_slice_in_dim(tokens, group * own_count, own_count, 0)
    hidden_state = own_tokens.astype(jnp.float32) + attention
    normed = rms_rows(hidden_state).astype(jnp.bfloat16)
    logits = jnp.dot(normed, router_weight, preferred_element_type=jnp.float32)
    expert_range = jnp.arange(experts, dtype=jnp.int32)
    matches = expert_ids[:, :, None] == expert_range[None, None, :]
    picked = jnp.sum(jnp.where(matches, logits[:, None, :], 0.0), axis=2)
    gates = jax.nn.softmax(picked, axis=1)
    gate_cols = jnp.sum(jnp.where(matches, gates[:, :, None], 0.0), axis=1)
    names = jnp.any(matches, axis=1).astype(jnp.int32)
    slot = jnp.cumsum(names, axis=0) - names
    slot_range = jnp.arange(capacity, dtype=jnp.int32)
    hits = (slot[:, :, None] == slot_range) & (names[:, :, None] > 0)
    send = jnp.einsum(
        "rec,rd->ecd", hits.astype(jnp.bfloat16), normed, preferred_element_type=jnp.float32
    ).astype(jnp.bfloat16)

    arrived = lax.all_to_all(send, "x", split_axis=0, concat_axis=0, tiled=True)
    arrived = arrived.reshape(experts * capacity, model_width)
    rows = lax.all_gather(arrived, ("c", "y", "z"), axis=0, tiled=True)
    line_rows = rows.shape[0] // nc
    other_rows = lax.dynamic_slice_in_dim(rows, (1 - ci) * line_rows, line_rows, 0)
    own_rows = lax.dynamic_slice_in_dim(rows, ci * line_rows, line_rows, 0)
    core_swap = [(i, i ^ 1) for i in range(nc)]
    other_out = expert_rows(other_rows, gate_weight, up_weight, down_weight)
    other_back = lax.ppermute(other_out, "c", core_swap)
    own_out = expert_rows(own_rows, gate_weight, up_weight, down_weight)
    summed = (own_out.astype(jnp.float32) + other_back.astype(jnp.float32)).astype(jnp.bfloat16)

    lines = summed.reshape(-1, experts * capacity, model_width)
    summed = jnp.sum(
        lax.all_to_all(lines, ("y", "z"), split_axis=0, concat_axis=0, tiled=True).astype(
            jnp.float32
        ),
        axis=0,
    )
    summed = summed.reshape(experts, capacity, model_width).astype(jnp.bfloat16)
    returned = lax.all_to_all(summed, "x", split_axis=0, concat_axis=0, tiled=True)

    weights = jnp.where(hits, gate_cols[:, :, None], 0.0)
    moe = jnp.einsum(
        "rec,ecd->rd", weights, returned.astype(jnp.float32), precision=lax.Precision.HIGHEST
    )
    return (hidden_state + moe).astype(jnp.bfloat16)


def solution(mesh):
    dp_size = mesh.shape["dp"]

    def run(*args):
        experts = args[6].shape[1]
        ex_size = mesh.shape["expert"]
        devices = np.asarray(mesh.devices).reshape(
            dp_size // CORES, CORES, experts, ex_size // experts
        )
        fine = Mesh(devices, ("z", "c", "x", "y"))
        tok = ("z", "c")
        grp = ("x", "y")
        placed = (
            P(tok, None),
            P(None, grp),
            P(None, grp),
            P(grp, None),
            P(),
            P(tok + grp, None),
            P(),
            P(None, grp + tok),
            P(None, grp + tok),
            P(grp + tok, None),
        )
        body = jax.shard_map(
            per_device, mesh=fine, in_specs=placed, out_specs=P(tok + grp, None), check_vma=False
        )
        return body(*args)

    return run
```

```python
import jax
import jax.numpy as jnp
import numpy as np
from jax import lax
from jax.sharding import Mesh
from jax.sharding import PartitionSpec as P

HD = 128
CORES = 2

EPSILON = 1e-05
ROPE_BASE = 1000000.0
MASKED_SCORE = -1e30


def rms_rows(matrix):
    matrix = matrix.astype(jnp.float32)
    return matrix * lax.rsqrt(jnp.mean(matrix * matrix, axis=-1, keepdims=True) + EPSILON)


def rotate(vectors, positions):
    half_width = vectors.shape[-1] // 2
    frequency = ROPE_BASE ** (-jnp.arange(half_width, dtype=jnp.float32) * 2.0 / vectors.shape[-1])
    angles = positions.astype(jnp.float32)[:, None] * frequency[None, :]
    cosine = jnp.cos(angles)[:, None, :]
    sine_part = jnp.sin(angles)[:, None, :]
    first_half = vectors[..., :half_width]
    second = vectors[..., half_width:]
    return jnp.concatenate(
        [first_half * cosine - second * sine_part, second * cosine + first_half * sine_part],
        axis=-1,
    )


def doc_layout(doc_lengths, positions):
    doc_ends = jnp.cumsum(doc_lengths)
    passed = (positions[:, None] >= doc_ends[None, :]).astype(jnp.int32)
    document = jnp.sum(passed, axis=1)
    doc_start = jnp.sum(passed * doc_lengths[None, :], axis=1)
    return (document, positions - doc_start)


def expert_rows(rows, gate_weight, up_weight, down_weight):
    gate_part = jnp.dot(rows, gate_weight, preferred_element_type=jnp.float32)
    up_part = jnp.dot(rows, up_weight, preferred_element_type=jnp.float32)
    activated = lax.optimization_barrier((jax.nn.silu(gate_part) * up_part).astype(jnp.bfloat16))
    return jnp.dot(activated, down_weight, preferred_element_type=jnp.float32).astype(jnp.bfloat16)


def per_device(
    tokens,
    query_weight,
    key_value_weight,
    out_weight,
    doc_lengths,
    expert_ids,
    router_weight,
    gate_weight,
    up_weight,
    down_weight,
):
    tok_dev, model_width = tokens.shape
    head_dim = HD
    per_group = query_weight.shape[1] // head_dim
    nx = lax.axis_size("x")
    ny = lax.axis_size("y")
    nc = lax.axis_size("c")
    xi = lax.axis_index("x")
    yi = lax.axis_index("y")
    zi = lax.axis_index("z")
    ci = lax.axis_index("c")
    shard = zi * nc + ci
    group = xi * ny + yi
    experts = router_weight.shape[1]
    own_count = tok_dev // (nx * ny)
    capacity = own_count * 3 // 4

    positions = shard * tok_dev + jnp.arange(tok_dev, dtype=jnp.int32)
    document, in_document = doc_layout(doc_lengths, positions)
    normed_in = rms_rows(tokens).astype(jnp.bfloat16)
    queries = jnp.dot(normed_in, query_weight, preferred_element_type=jnp.float32).reshape(
        tok_dev, per_group, head_dim
    )
    queries = rotate(queries, in_document).astype(jnp.bfloat16)
    half_part = jnp.dot(normed_in, key_value_weight, preferred_element_type=jnp.float32)
    rotated = rotate(half_part[:, None, :], in_document)[:, 0, :]
    holds_keys = group % 2 == 0
    mine = jnp.where(holds_keys, rotated, half_part).astype(jnp.bfloat16)
    pairs = [(i, i ^ 1) for i in range(ny)]
    partner = lax.ppermute(mine, "y", pairs)
    key_rows = jnp.where(holds_keys, mine, partner)
    values = jnp.where(holds_keys, partner, mine)
    both = jnp.stack([key_rows, values], axis=0)
    nz = lax.axis_size("z")
    core_swap = [(i, i ^ 1) for i in range(nc)]
    other_core = lax.ppermute(both, "c", core_swap)
    pair = jnp.where(ci == 0, jnp.stack([both, other_core]), jnp.stack([other_core, both]))
    ring = [pair] + [
        lax.ppermute(pair, "z", [(i, (i - k) % nz) for i in range(nz)]) for k in range(1, nz)
    ]
    gathered = jnp.stack(ring).transpose(2, 0, 1, 3, 4).reshape(2, -1, head_dim)
    key_piece = gathered[0]
    value_piece = gathered[1]
    ring_range = jnp.arange(nz, dtype=jnp.int32)
    shard_of = ((zi + ring_range) % nz)[:, None] * nc + jnp.arange(nc, dtype=jnp.int32)[None, :]
    key_places = (
        shard_of[:, :, None] * tok_dev + jnp.arange(tok_dev, dtype=jnp.int32)[None, None, :]
    ).reshape(-1)
    key_doc, unused = doc_layout(doc_lengths, key_places)
    allowed = (document[:, None] == key_doc[None, :]) & (key_places[None, :] <= positions[:, None])
    scores = (
        jnp.einsum("tqd,jd->tqj", queries, key_piece, preferred_element_type=jnp.float32)
        * head_dim ** (-0.5)
    )
    masked = jnp.where(allowed[:, None, :], scores, MASKED_SCORE)
    row_max = jnp.max(masked, axis=2)
    expo = jnp.where(allowed[:, None, :], jnp.exp(masked - row_max[..., None]), 0.0)
    denom = jnp.sum(expo, axis=2)
    weighted = jnp.einsum(
        "tqj,jd->tqd", expo.astype(jnp.bfloat16), value_piece, preferred_element_type=jnp.float32
    )
    context = (
        (weighted / denom[..., None]).astype(jnp.bfloat16).reshape(tok_dev, per_group * head_dim)
    )
    partial_value = jnp.dot(context, out_weight, preferred_element_type=jnp.float32)
    blocks = partial_value.astype(jnp.bfloat16).reshape(nx * ny, own_count, model_width)
    attention = jnp.sum(
        lax.all_to_all(blocks, ("x", "y"), split_axis=0, concat_axis=0, tiled=True).astype(
            jnp.float32
        ),
        axis=0,
    )

    own_tokens = lax.dynamic_slice_in_dim(tokens, group * own_count, own_count, 0)
    hidden_state = own_tokens.astype(jnp.float32) + attention
    normed = rms_rows(hidden_state).astype(jnp.bfloat16)
    logits = jnp.dot(normed, router_weight, preferred_element_type=jnp.float32)
    expert_range = jnp.arange(experts, dtype=jnp.int32)
    matches = expert_ids[:, :, None] == expert_range[None, None, :]
    picked = jnp.sum(jnp.where(matches, logits[:, None, :], 0.0), axis=2)
    gates = jax.nn.softmax(picked, axis=1)
    gate_cols = jnp.sum(jnp.where(matches, gates[:, :, None], 0.0), axis=1)
    names = jnp.any(matches, axis=1).astype(jnp.int32)
    slot = jnp.cumsum(names, axis=0) - names
    slot_range = jnp.arange(capacity, dtype=jnp.int32)
    hits = (slot[:, :, None] == slot_range) & (names[:, :, None] > 0)
    shift = (xi + jnp.arange(nx, dtype=jnp.int32)) % nx
    hits = jnp.take(hits, shift, axis=1)
    gate_cols = jnp.take(gate_cols, shift, axis=1)
    send = jnp.einsum(
        "rec,rd->ecd", hits.astype(jnp.bfloat16), normed, preferred_element_type=jnp.float32
    ).astype(jnp.bfloat16)

    arrived = [send[0]] + [
        lax.ppermute(send[k], "x", [(i, (i + k) % nx) for i in range(nx)]) for k in range(1, nx)
    ]
    arrived = jnp.concatenate(arrived, axis=0)
    rows = lax.all_gather(arrived, ("c", "y", "z"), axis=0, tiled=True)
    line_rows = rows.shape[0] // nc
    other_rows = lax.dynamic_slice_in_dim(rows, (1 - ci) * line_rows, line_rows, 0)
    own_rows = lax.dynamic_slice_in_dim(rows, ci * line_rows, line_rows, 0)
    other_out = expert_rows(other_rows, gate_weight, up_weight, down_weight)
    other_back = lax.ppermute(other_out, "c", core_swap)
    own_out = expert_rows(own_rows, gate_weight, up_weight, down_weight)
    summed = (own_out.astype(jnp.float32) + other_back.astype(jnp.float32)).astype(jnp.bfloat16)

    lines = summed.reshape(-1, experts * capacity, model_width)
    summed = jnp.sum(
        lax.all_to_all(lines, ("y", "z"), split_axis=0, concat_axis=0, tiled=True).astype(
            jnp.float32
        ),
        axis=0,
    )
    summed = summed.reshape(experts, capacity, model_width).astype(jnp.bfloat16)
    returned = jnp.stack(
        [summed[0]]
        + [
            lax.ppermute(summed[k], "x", [(i, (i - k) % nx) for i in range(nx)])
            for k in range(1, nx)
        ]
    )

    weights = jnp.where(hits, gate_cols[:, :, None], 0.0)
    moe = jnp.einsum(
        "rec,ecd->rd", weights, returned.astype(jnp.float32), precision=lax.Precision.HIGHEST
    )
    return (hidden_state + moe).astype(jnp.bfloat16)


def solution(mesh):
    dp_size = mesh.shape["dp"]

    def run(*args):
        experts = args[6].shape[1]
        ex_size = mesh.shape["expert"]
        devices = np.asarray(mesh.devices).reshape(
            dp_size // CORES, CORES, experts, ex_size // experts
        )
        fine = Mesh(devices, ("z", "c", "x", "y"))
        tok = ("z", "c")
        grp = ("x", "y")
        placed = (
            P(tok, None),
            P(None, grp),
            P(None, grp),
            P(grp, None),
            P(),
            P(tok + grp, None),
            P(),
            P(None, grp + tok),
            P(None, grp + tok),
            P(grp + tok, None),
        )
        body = jax.shard_map(
            per_device, mesh=fine, in_specs=placed, out_specs=P(tok + grp, None), check_vma=False
        )
        return body(*args)

    return run
```

```python
import jax
import jax.numpy as jnp
import numpy as np
from jax import lax
from jax.sharding import Mesh
from jax.sharding import PartitionSpec as P

HD = 128
CORES = 2

EPSILON = 1e-05
ROPE_BASE = 1000000.0
MASKED_SCORE = -1e30


def rms_rows(matrix):
    matrix = matrix.astype(jnp.float32)
    return matrix * lax.rsqrt(jnp.mean(matrix * matrix, axis=-1, keepdims=True) + EPSILON)


def rotate(vectors, positions):
    half_width = vectors.shape[-1] // 2
    frequency = ROPE_BASE ** (-jnp.arange(half_width, dtype=jnp.float32) * 2.0 / vectors.shape[-1])
    angles = positions.astype(jnp.float32)[:, None] * frequency[None, :]
    cosine = jnp.cos(angles)[:, None, :]
    sine_part = jnp.sin(angles)[:, None, :]
    first_half = vectors[..., :half_width]
    second = vectors[..., half_width:]
    return jnp.concatenate(
        [first_half * cosine - second * sine_part, second * cosine + first_half * sine_part],
        axis=-1,
    )


def doc_layout(doc_lengths, positions):
    doc_ends = jnp.cumsum(doc_lengths)
    passed = (positions[:, None] >= doc_ends[None, :]).astype(jnp.int32)
    document = jnp.sum(passed, axis=1)
    doc_start = jnp.sum(passed * doc_lengths[None, :], axis=1)
    return (document, positions - doc_start)


def expert_rows(rows, gate_weight, up_weight, down_weight):
    gate_part = jnp.dot(rows, gate_weight, preferred_element_type=jnp.float32)
    up_part = jnp.dot(rows, up_weight, preferred_element_type=jnp.float32)
    activated = lax.optimization_barrier((jax.nn.silu(gate_part) * up_part).astype(jnp.bfloat16))
    return jnp.dot(activated, down_weight, preferred_element_type=jnp.float32).astype(jnp.bfloat16)


def per_device(
    tokens,
    query_weight,
    key_value_weight,
    out_weight,
    doc_lengths,
    expert_ids,
    router_weight,
    gate_weight,
    up_weight,
    down_weight,
):
    tok_dev, model_width = tokens.shape
    head_dim = HD
    per_group = query_weight.shape[1] // head_dim
    nx = lax.axis_size("x")
    ny = lax.axis_size("y")
    nc = lax.axis_size("c")
    xi = lax.axis_index("x")
    yi = lax.axis_index("y")
    zi = lax.axis_index("z")
    ci = lax.axis_index("c")
    shard = zi * nc + ci
    group = xi * ny + yi
    experts = router_weight.shape[1]
    own_count = tok_dev // (nx * ny)
    capacity = own_count * 3 // 4

    positions = shard * tok_dev + jnp.arange(tok_dev, dtype=jnp.int32)
    document, in_document = doc_layout(doc_lengths, positions)
    normed_in = rms_rows(tokens).astype(jnp.bfloat16)
    queries = jnp.dot(normed_in, query_weight, preferred_element_type=jnp.float32).reshape(
        tok_dev, per_group, head_dim
    )
    queries = rotate(queries, in_document).astype(jnp.bfloat16)
    half_part = jnp.dot(normed_in, key_value_weight, preferred_element_type=jnp.float32)
    rotated = rotate(half_part[:, None, :], in_document)[:, 0, :]
    holds_keys = group % 2 == 0
    mine = jnp.where(holds_keys, rotated, half_part).astype(jnp.bfloat16)
    pairs = [(i, i ^ 1) for i in range(ny)]
    partner = lax.ppermute(mine, "y", pairs)
    key_rows = jnp.where(holds_keys, mine, partner)
    values = jnp.where(holds_keys, partner, mine)
    both = jnp.stack([key_rows, values], axis=0)
    nz = lax.axis_size("z")
    core_swap = [(i, i ^ 1) for i in range(nc)]
    other_core = lax.ppermute(both, "c", core_swap)
    pair = jnp.where(ci == 0, jnp.stack([both, other_core]), jnp.stack([other_core, both]))
    ring = [pair] + [
        lax.ppermute(pair, "z", [(i, (i - k) % nz) for i in range(nz)]) for k in range(1, nz)
    ]
    gathered = jnp.stack(ring).transpose(2, 0, 1, 3, 4).reshape(2, -1, head_dim)
    key_piece = gathered[0]
    value_piece = gathered[1]
    ring_range = jnp.arange(nz, dtype=jnp.int32)
    shard_of = ((zi + ring_range) % nz)[:, None] * nc + jnp.arange(nc, dtype=jnp.int32)[None, :]
    key_places = (
        shard_of[:, :, None] * tok_dev + jnp.arange(tok_dev, dtype=jnp.int32)[None, None, :]
    ).reshape(-1)
    key_doc, unused = doc_layout(doc_lengths, key_places)
    allowed = (document[:, None] == key_doc[None, :]) & (key_places[None, :] <= positions[:, None])
    scores = (
        jnp.einsum("tqd,jd->tqj", queries, key_piece, preferred_element_type=jnp.float32)
        * head_dim ** (-0.5)
    )
    masked = jnp.where(allowed[:, None, :], scores, MASKED_SCORE)
    row_max = jnp.max(masked, axis=2)
    expo = jnp.where(allowed[:, None, :], jnp.exp(masked - row_max[..., None]), 0.0)
    denom = jnp.sum(expo, axis=2)
    weighted = jnp.einsum(
        "tqj,jd->tqd", expo.astype(jnp.bfloat16), value_piece, preferred_element_type=jnp.float32
    )
    context = (
        (weighted / denom[..., None]).astype(jnp.bfloat16).reshape(tok_dev, per_group * head_dim)
    )
    partial_value = jnp.dot(context, out_weight, preferred_element_type=jnp.float32)
    blocks = partial_value.astype(jnp.bfloat16).reshape(nx * ny, own_count, model_width)
    attention = jnp.sum(
        lax.all_to_all(blocks, ("x", "y"), split_axis=0, concat_axis=0, tiled=True).astype(
            jnp.float32
        ),
        axis=0,
    )

    own_tokens = lax.dynamic_slice_in_dim(tokens, group * own_count, own_count, 0)
    hidden_state = own_tokens.astype(jnp.float32) + attention
    normed = rms_rows(hidden_state).astype(jnp.bfloat16)
    logits = jnp.dot(normed, router_weight, preferred_element_type=jnp.float32)
    expert_range = jnp.arange(experts, dtype=jnp.int32)
    matches = expert_ids[:, :, None] == expert_range[None, None, :]
    picked = jnp.sum(jnp.where(matches, logits[:, None, :], 0.0), axis=2)
    gates = jax.nn.softmax(picked, axis=1)
    gate_cols = jnp.sum(jnp.where(matches, gates[:, :, None], 0.0), axis=1)
    names = jnp.any(matches, axis=1).astype(jnp.int32)
    slot = jnp.cumsum(names, axis=0) - names
    slot_range = jnp.arange(capacity, dtype=jnp.int32)
    hits = (slot[:, :, None] == slot_range) & (names[:, :, None] > 0)
    shift = (xi + jnp.arange(nx, dtype=jnp.int32)) % nx
    hits = jnp.take(hits, shift, axis=1)
    gate_cols = jnp.take(gate_cols, shift, axis=1)
    send = jnp.einsum(
        "rec,rd->ecd", hits.astype(jnp.bfloat16), normed, preferred_element_type=jnp.float32
    ).astype(jnp.bfloat16)

    arrived = [send[0]] + [
        lax.ppermute(send[k], "x", [(i, (i + k) % nx) for i in range(nx)]) for k in range(1, nx)
    ]
    arrived = jnp.concatenate(arrived, axis=0)
    rows = lax.all_gather(arrived, ("c", "y", "z"), axis=0, tiled=True)
    line_rows = rows.shape[0] // nc
    other_rows = lax.dynamic_slice_in_dim(rows, (1 - ci) * line_rows, line_rows, 0)
    own_rows = lax.dynamic_slice_in_dim(rows, ci * line_rows, line_rows, 0)
    other_out = expert_rows(other_rows, gate_weight, up_weight, down_weight)
    other_back = lax.ppermute(other_out, "c", core_swap)
    own_out = expert_rows(own_rows, gate_weight, up_weight, down_weight)
    summed = (own_out.astype(jnp.float32) + other_back.astype(jnp.float32)).astype(jnp.bfloat16)

    split = model_width * 2 // 3 // 128 * 128
    lines = summed[:, :split].reshape(-1, experts * capacity, split)
    spread = lax.all_to_all(lines, ("y", "z"), split_axis=0, concat_axis=0, tiled=True)
    scattered = lax.psum_scatter(summed[:, split:], ("y", "z"), scatter_dimension=0, tiled=True)
    summed = jnp.concatenate(
        [jnp.sum(spread.astype(jnp.float32), axis=0), scattered.astype(jnp.float32)], axis=1
    )
    summed = summed.reshape(experts, capacity, model_width).astype(jnp.bfloat16)
    returned = jnp.stack(
        [summed[0]]
        + [
            lax.ppermute(summed[k], "x", [(i, (i - k) % nx) for i in range(nx)])
            for k in range(1, nx)
        ]
    )

    weights = jnp.where(hits, gate_cols[:, :, None], 0.0)
    moe = jnp.einsum(
        "rec,ecd->rd", weights, returned.astype(jnp.float32), precision=lax.Precision.HIGHEST
    )
    return (hidden_state + moe).astype(jnp.bfloat16)


def solution(mesh):
    dp_size = mesh.shape["dp"]

    def run(*args):
        experts = args[6].shape[1]
        ex_size = mesh.shape["expert"]
        devices = np.asarray(mesh.devices).reshape(
            dp_size // CORES, CORES, experts, ex_size // experts
        )
        fine = Mesh(devices, ("z", "c", "x", "y"))
        tok = ("z", "c")
        grp = ("x", "y")
        placed = (
            P(tok, None),
            P(None, grp),
            P(None, grp),
            P(grp, None),
            P(),
            P(tok + grp, None),
            P(),
            P(None, grp + tok),
            P(None, grp + tok),
            P(grp + tok, None),
        )
        body = jax.shard_map(
            per_device, mesh=fine, in_specs=placed, out_specs=P(tok + grp, None), check_vma=False
        )
        return body(*args)

    return run
```

```python
import jax
import jax.numpy as jnp
import numpy as np
from jax import lax
from jax.sharding import Mesh
from jax.sharding import PartitionSpec as P

HD = 128
CORES = 2

EPSILON = 1e-05
ROPE_BASE = 1000000.0
MASKED_SCORE = -1e30


def rms_rows(matrix):
    matrix = matrix.astype(jnp.float32)
    return matrix * lax.rsqrt(jnp.mean(matrix * matrix, axis=-1, keepdims=True) + EPSILON)


def rotate(vectors, positions):
    half_width = vectors.shape[-1] // 2
    frequency = ROPE_BASE ** (-jnp.arange(half_width, dtype=jnp.float32) * 2.0 / vectors.shape[-1])
    angles = positions.astype(jnp.float32)[:, None] * frequency[None, :]
    cosine = jnp.cos(angles)[:, None, :]
    sine_part = jnp.sin(angles)[:, None, :]
    first_half = vectors[..., :half_width]
    second = vectors[..., half_width:]
    return jnp.concatenate(
        [first_half * cosine - second * sine_part, second * cosine + first_half * sine_part],
        axis=-1,
    )


def doc_layout(doc_lengths, positions):
    doc_ends = jnp.cumsum(doc_lengths)
    passed = (positions[:, None] >= doc_ends[None, :]).astype(jnp.int32)
    document = jnp.sum(passed, axis=1)
    doc_start = jnp.sum(passed * doc_lengths[None, :], axis=1)
    return (document, positions - doc_start)


def expert_rows(rows, gate_up_weight, down_weight):
    hidden = down_weight.shape[0]
    both = jnp.dot(rows, gate_up_weight, preferred_element_type=jnp.float32)
    gate_part = both[:, :hidden]
    up_part = both[:, hidden:]
    activated = lax.optimization_barrier((jax.nn.silu(gate_part) * up_part).astype(jnp.bfloat16))
    return jnp.dot(activated, down_weight, preferred_element_type=jnp.float32).astype(jnp.bfloat16)


def per_device(
    tokens,
    query_weight,
    key_value_weight,
    out_weight,
    doc_lengths,
    expert_ids,
    router_weight,
    gate_weight,
    up_weight,
    down_weight,
):
    tok_dev, model_width = tokens.shape
    head_dim = HD
    per_group = query_weight.shape[1] // head_dim
    nx = lax.axis_size("x")
    ny = lax.axis_size("y")
    nc = lax.axis_size("c")
    xi = lax.axis_index("x")
    yi = lax.axis_index("y")
    zi = lax.axis_index("z")
    ci = lax.axis_index("c")
    shard = zi * nc + ci
    group = xi * ny + yi
    experts = router_weight.shape[1]
    own_count = tok_dev // (nx * ny)
    capacity = own_count * 3 // 4

    positions = shard * tok_dev + jnp.arange(tok_dev, dtype=jnp.int32)
    document, in_document = doc_layout(doc_lengths, positions)
    normed_in = rms_rows(tokens).astype(jnp.bfloat16)
    queries = jnp.dot(normed_in, query_weight, preferred_element_type=jnp.float32).reshape(
        tok_dev, per_group, head_dim
    )
    queries = rotate(queries, in_document).astype(jnp.bfloat16)
    half_part = jnp.dot(normed_in, key_value_weight, preferred_element_type=jnp.float32)
    rotated = rotate(half_part[:, None, :], in_document)[:, 0, :]
    holds_keys = group % 2 == 0
    mine = jnp.where(holds_keys, rotated, half_part).astype(jnp.bfloat16)
    pairs = [(i, i ^ 1) for i in range(ny)]
    partner = lax.ppermute(mine, "y", pairs)
    key_rows = jnp.where(holds_keys, mine, partner)
    values = jnp.where(holds_keys, partner, mine)
    both = jnp.stack([key_rows, values], axis=0)
    nz = lax.axis_size("z")
    core_swap = [(i, i ^ 1) for i in range(nc)]
    other_core = lax.ppermute(both, "c", core_swap)
    pair = jnp.where(ci == 0, jnp.stack([both, other_core]), jnp.stack([other_core, both]))
    ring = [pair] + [
        lax.ppermute(pair, "z", [(i, (i - k) % nz) for i in range(nz)]) for k in range(1, nz)
    ]
    gathered = jnp.stack(ring).transpose(2, 0, 1, 3, 4).reshape(2, -1, head_dim)
    key_piece = gathered[0]
    value_piece = gathered[1]
    ring_range = jnp.arange(nz, dtype=jnp.int32)
    shard_of = ((zi + ring_range) % nz)[:, None] * nc + jnp.arange(nc, dtype=jnp.int32)[None, :]
    key_places = (
        shard_of[:, :, None] * tok_dev + jnp.arange(tok_dev, dtype=jnp.int32)[None, None, :]
    ).reshape(-1)
    key_doc, unused = doc_layout(doc_lengths, key_places)
    allowed = (document[:, None] == key_doc[None, :]) & (key_places[None, :] <= positions[:, None])
    scores = (
        jnp.einsum("tqd,jd->tqj", queries, key_piece, preferred_element_type=jnp.float32)
        * head_dim ** (-0.5)
    )
    masked = jnp.where(allowed[:, None, :], scores, MASKED_SCORE)
    row_max = jnp.max(masked, axis=2)
    expo = jnp.where(allowed[:, None, :], jnp.exp(masked - row_max[..., None]), 0.0)
    denom = jnp.sum(expo, axis=2)
    weighted = jnp.einsum(
        "tqj,jd->tqd", expo.astype(jnp.bfloat16), value_piece, preferred_element_type=jnp.float32
    )
    context = (
        (weighted / denom[..., None]).astype(jnp.bfloat16).reshape(tok_dev, per_group * head_dim)
    )
    partial_value = jnp.dot(context, out_weight, preferred_element_type=jnp.float32)
    blocks = partial_value.astype(jnp.bfloat16).reshape(nx * ny, own_count, model_width)
    attention = jnp.sum(
        lax.all_to_all(blocks, ("x", "y"), split_axis=0, concat_axis=0, tiled=True).astype(
            jnp.float32
        ),
        axis=0,
    )

    own_tokens = lax.dynamic_slice_in_dim(tokens, group * own_count, own_count, 0)
    hidden_state = own_tokens.astype(jnp.float32) + attention
    normed = rms_rows(hidden_state).astype(jnp.bfloat16)
    logits = jnp.dot(normed, router_weight, preferred_element_type=jnp.float32)
    expert_range = jnp.arange(experts, dtype=jnp.int32)
    matches = expert_ids[:, :, None] == expert_range[None, None, :]
    picked = jnp.sum(jnp.where(matches, logits[:, None, :], 0.0), axis=2)
    gates = jax.nn.softmax(picked, axis=1)
    gate_cols = jnp.sum(jnp.where(matches, gates[:, :, None], 0.0), axis=1)
    names = jnp.any(matches, axis=1).astype(jnp.int32)
    slot = jnp.cumsum(names, axis=0) - names
    slot_range = jnp.arange(capacity, dtype=jnp.int32)
    hits = (slot[:, :, None] == slot_range) & (names[:, :, None] > 0)
    shift = (xi + jnp.arange(nx, dtype=jnp.int32)) % nx
    hits = jnp.take(hits, shift, axis=1)
    gate_cols = jnp.take(gate_cols, shift, axis=1)
    send = jnp.einsum(
        "rec,rd->ecd", hits.astype(jnp.bfloat16), normed, preferred_element_type=jnp.float32
    ).astype(jnp.bfloat16)

    arrived = [send[0]] + [
        lax.ppermute(send[k], "x", [(i, (i + k) % nx) for i in range(nx)]) for k in range(1, nx)
    ]
    arrived = jnp.concatenate(arrived, axis=0)
    rows = lax.all_gather(arrived, ("c", "y", "z"), axis=0, tiled=True)
    gate_up_weight = jnp.concatenate([gate_weight, up_weight], axis=1)
    line_rows = rows.shape[0] // nc
    other_rows = lax.dynamic_slice_in_dim(rows, (1 - ci) * line_rows, line_rows, 0)
    own_rows = lax.dynamic_slice_in_dim(rows, ci * line_rows, line_rows, 0)
    other_out = expert_rows(other_rows, gate_up_weight, down_weight)
    other_back = lax.ppermute(other_out, "c", core_swap)
    own_out = expert_rows(own_rows, gate_up_weight, down_weight)
    summed = (own_out.astype(jnp.float32) + other_back.astype(jnp.float32)).astype(jnp.bfloat16)

    lines = summed.reshape(-1, experts * capacity, model_width)
    summed = jnp.sum(
        lax.all_to_all(lines, ("y", "z"), split_axis=0, concat_axis=0, tiled=True).astype(
            jnp.float32
        ),
        axis=0,
    )
    summed = summed.reshape(experts, capacity, model_width).astype(jnp.bfloat16)
    returned = jnp.stack(
        [summed[0]]
        + [
            lax.ppermute(summed[k], "x", [(i, (i - k) % nx) for i in range(nx)])
            for k in range(1, nx)
        ]
    )

    weights = jnp.where(hits, gate_cols[:, :, None], 0.0)
    moe = jnp.einsum(
        "rec,ecd->rd", weights, returned.astype(jnp.float32), precision=lax.Precision.HIGHEST
    )
    return (hidden_state + moe).astype(jnp.bfloat16)


def solution(mesh):
    dp_size = mesh.shape["dp"]

    def run(*args):
        experts = args[6].shape[1]
        ex_size = mesh.shape["expert"]
        devices = np.asarray(mesh.devices).reshape(
            dp_size // CORES, CORES, experts, ex_size // experts
        )
        fine = Mesh(devices, ("z", "c", "x", "y"))
        tok = ("z", "c")
        grp = ("x", "y")
        placed = (
            P(tok, None),
            P(None, grp),
            P(None, grp),
            P(grp, None),
            P(),
            P(tok + grp, None),
            P(),
            P(None, grp + tok),
            P(None, grp + tok),
            P(grp + tok, None),
        )
        body = jax.shard_map(
            per_device, mesh=fine, in_specs=placed, out_specs=P(tok + grp, None), check_vma=False
        )
        return body(*args)

    return run
```

```python
import jax
import jax.numpy as jnp
import numpy as np
from jax import lax
from jax.sharding import Mesh
from jax.sharding import PartitionSpec as P

HD = 128
CORES = 2

EPSILON = 1e-05
ROPE_BASE = 1000000.0
MASKED_SCORE = -1e30


def rms_rows(matrix):
    matrix = matrix.astype(jnp.float32)
    return matrix * lax.rsqrt(jnp.mean(matrix * matrix, axis=-1, keepdims=True) + EPSILON)


def rotate(vectors, positions):
    half_width = vectors.shape[-1] // 2
    frequency = ROPE_BASE ** (-jnp.arange(half_width, dtype=jnp.float32) * 2.0 / vectors.shape[-1])
    angles = positions.astype(jnp.float32)[:, None] * frequency[None, :]
    cosine = jnp.cos(angles)[:, None, :]
    sine_part = jnp.sin(angles)[:, None, :]
    first_half = vectors[..., :half_width]
    second = vectors[..., half_width:]
    return jnp.concatenate(
        [first_half * cosine - second * sine_part, second * cosine + first_half * sine_part],
        axis=-1,
    )


def doc_layout(doc_lengths, positions):
    doc_ends = jnp.cumsum(doc_lengths)
    passed = (positions[:, None] >= doc_ends[None, :]).astype(jnp.int32)
    document = jnp.sum(passed, axis=1)
    doc_start = jnp.sum(passed * doc_lengths[None, :], axis=1)
    return (document, positions - doc_start)


def expert_rows(rows, gate_up_weight, down_weight):
    hidden = down_weight.shape[0]
    both = jnp.dot(rows, gate_up_weight, preferred_element_type=jnp.float32)
    gate_part = both[:, :hidden]
    up_part = both[:, hidden:]
    activated = lax.optimization_barrier((jax.nn.silu(gate_part) * up_part).astype(jnp.bfloat16))
    return jnp.dot(activated, down_weight, preferred_element_type=jnp.float32).astype(jnp.bfloat16)


def per_device(
    tokens,
    query_weight,
    key_value_weight,
    out_weight,
    doc_lengths,
    expert_ids,
    router_weight,
    gate_weight,
    up_weight,
    down_weight,
):
    tok_dev, model_width = tokens.shape
    head_dim = HD
    per_group = query_weight.shape[1] // head_dim
    nx = lax.axis_size("x")
    ny = lax.axis_size("y")
    nc = lax.axis_size("c")
    xi = lax.axis_index("x")
    yi = lax.axis_index("y")
    zi = lax.axis_index("z")
    ci = lax.axis_index("c")
    shard = zi * nc + ci
    group = xi * ny + yi
    experts = router_weight.shape[1]
    own_count = tok_dev // (nx * ny)
    capacity = own_count * 3 // 4

    positions = shard * tok_dev + jnp.arange(tok_dev, dtype=jnp.int32)
    document, in_document = doc_layout(doc_lengths, positions)
    normed_in = rms_rows(tokens).astype(jnp.bfloat16)
    queries = jnp.dot(normed_in, query_weight, preferred_element_type=jnp.float32).reshape(
        tok_dev, per_group, head_dim
    )
    queries = rotate(queries, in_document).astype(jnp.bfloat16)
    half_part = jnp.dot(normed_in, key_value_weight, preferred_element_type=jnp.float32)
    rotated = rotate(half_part[:, None, :], in_document)[:, 0, :]
    holds_keys = group % 2 == 0
    mine = jnp.where(holds_keys, rotated, half_part).astype(jnp.bfloat16)
    pairs = [(i, i ^ 1) for i in range(ny)]
    partner = lax.ppermute(mine, "y", pairs)
    key_rows = jnp.where(holds_keys, mine, partner)
    values = jnp.where(holds_keys, partner, mine)
    both = jnp.stack([key_rows, values], axis=0)
    nz = lax.axis_size("z")
    core_swap = [(i, i ^ 1) for i in range(nc)]
    other_core = lax.ppermute(both, "c", core_swap)
    pair = jnp.where(ci == 0, jnp.stack([both, other_core]), jnp.stack([other_core, both]))
    ring = [pair] + [
        lax.ppermute(pair, "z", [(i, (i - k) % nz) for i in range(nz)]) for k in range(1, nz)
    ]
    gathered = jnp.stack(ring).transpose(2, 0, 1, 3, 4).reshape(2, -1, head_dim)
    key_piece = gathered[0]
    value_piece = gathered[1]
    ring_range = jnp.arange(nz, dtype=jnp.int32)
    shard_of = ((zi + ring_range) % nz)[:, None] * nc + jnp.arange(nc, dtype=jnp.int32)[None, :]
    key_places = (
        shard_of[:, :, None] * tok_dev + jnp.arange(tok_dev, dtype=jnp.int32)[None, None, :]
    ).reshape(-1)
    key_doc, unused = doc_layout(doc_lengths, key_places)
    allowed = (document[:, None] == key_doc[None, :]) & (key_places[None, :] <= positions[:, None])
    scores = (
        jnp.einsum("tqd,jd->tqj", queries, key_piece, preferred_element_type=jnp.float32)
        * head_dim ** (-0.5)
    )
    masked = jnp.where(allowed[:, None, :], scores, MASKED_SCORE)
    row_max = jnp.max(masked, axis=2)
    expo = jnp.where(allowed[:, None, :], jnp.exp(masked - row_max[..., None]), 0.0)
    denom = jnp.sum(expo, axis=2)
    weighted = jnp.einsum(
        "tqj,jd->tqd", expo.astype(jnp.bfloat16), value_piece, preferred_element_type=jnp.float32
    )
    context = (
        (weighted / denom[..., None]).astype(jnp.bfloat16).reshape(tok_dev, per_group * head_dim)
    )
    partial_value = jnp.dot(context, out_weight, preferred_element_type=jnp.float32)
    blocks = partial_value.astype(jnp.bfloat16).reshape(nx * ny, own_count, model_width)
    attention = jnp.sum(
        lax.all_to_all(blocks, ("x", "y"), split_axis=0, concat_axis=0, tiled=True).astype(
            jnp.float32
        ),
        axis=0,
    )

    own_tokens = lax.dynamic_slice_in_dim(tokens, group * own_count, own_count, 0)
    hidden_state = own_tokens.astype(jnp.float32) + attention
    normed = rms_rows(hidden_state).astype(jnp.bfloat16)
    logits = jnp.dot(normed, router_weight, preferred_element_type=jnp.float32)
    expert_range = jnp.arange(experts, dtype=jnp.int32)
    matches = expert_ids[:, :, None] == expert_range[None, None, :]
    picked = jnp.sum(jnp.where(matches, logits[:, None, :], 0.0), axis=2)
    gates = jax.nn.softmax(picked, axis=1)
    gate_cols = jnp.sum(jnp.where(matches, gates[:, :, None], 0.0), axis=1)
    names = jnp.any(matches, axis=1).astype(jnp.int32)
    slot = jnp.cumsum(names, axis=0) - names
    slot_range = jnp.arange(capacity, dtype=jnp.int32)
    hits = (slot[:, :, None] == slot_range) & (names[:, :, None] > 0)
    shift = (xi + jnp.arange(nx, dtype=jnp.int32)) % nx
    send = jnp.einsum(
        "rec,rd->ecd",
        jnp.take(hits, shift, axis=1).astype(jnp.bfloat16),
        normed,
        preferred_element_type=jnp.float32,
    ).astype(jnp.bfloat16)

    arrived = [send[0]] + [
        lax.ppermute(send[k], "x", [(i, (i + k) % nx) for i in range(nx)]) for k in range(1, nx)
    ]
    arrived = jnp.stack(arrived)
    arrived = jnp.take(arrived, (xi - jnp.arange(nx, dtype=jnp.int32)) % nx, axis=0)
    arrived = arrived.reshape(experts * capacity, model_width)
    rows = lax.all_gather(arrived, ("c", "y", "z"), axis=0, tiled=True)
    gate_up_weight = jnp.concatenate([gate_weight, up_weight], axis=1)
    line_rows = rows.shape[0] // nc
    other_rows = lax.dynamic_slice_in_dim(rows, (1 - ci) * line_rows, line_rows, 0)
    own_rows = lax.dynamic_slice_in_dim(rows, ci * line_rows, line_rows, 0)
    other_out = expert_rows(other_rows, gate_up_weight, down_weight)
    other_back = lax.ppermute(other_out, "c", core_swap)
    own_out = expert_rows(own_rows, gate_up_weight, down_weight)
    summed = (own_out.astype(jnp.float32) + other_back.astype(jnp.float32)).astype(jnp.bfloat16)

    lines = summed.reshape(-1, capacity, model_width)
    spread = lax.all_to_all(lines, ("y", "z", "x"), split_axis=0, concat_axis=0, tiled=True)
    returned = jnp.sum(
        spread.reshape(-1, experts, capacity, model_width).astype(jnp.float32), axis=0
    )

    weights = jnp.where(hits, gate_cols[:, :, None], 0.0)
    moe = jnp.einsum(
        "rec,ecd->rd", weights, returned, precision=lax.Precision.HIGHEST
    )
    return (hidden_state + moe).astype(jnp.bfloat16)


def solution(mesh):
    dp_size = mesh.shape["dp"]

    def run(*args):
        experts = args[6].shape[1]
        ex_size = mesh.shape["expert"]
        devices = np.asarray(mesh.devices).reshape(
            dp_size // CORES, CORES, experts, ex_size // experts
        )
        fine = Mesh(devices, ("z", "c", "x", "y"))
        tok = ("z", "c")
        grp = ("x", "y")
        placed = (
            P(tok, None),
            P(None, grp),
            P(None, grp),
            P(grp, None),
            P(),
            P(tok + grp, None),
            P(),
            P(None, grp + tok),
            P(None, grp + tok),
            P(grp + tok, None),
        )
        body = jax.shard_map(
            per_device, mesh=fine, in_specs=placed, out_specs=P(tok + grp, None), check_vma=False
        )
        return body(*args)

    return run
```

```python
import jax
import jax.numpy as jnp
import numpy as np
from jax import lax
from jax.sharding import Mesh
from jax.sharding import PartitionSpec as P

HD = 128
CORES = 2

EPSILON = 1e-05
ROPE_BASE = 1000000.0
MASKED_SCORE = -1e30


def rms_rows(matrix):
    matrix = matrix.astype(jnp.float32)
    return matrix * lax.rsqrt(jnp.mean(matrix * matrix, axis=-1, keepdims=True) + EPSILON)


def rotate(vectors, positions):
    half_width = vectors.shape[-1] // 2
    frequency = ROPE_BASE ** (-jnp.arange(half_width, dtype=jnp.float32) * 2.0 / vectors.shape[-1])
    angles = positions.astype(jnp.float32)[:, None] * frequency[None, :]
    cosine = jnp.cos(angles)[:, None, :]
    sine_part = jnp.sin(angles)[:, None, :]
    first_half = vectors[..., :half_width]
    second = vectors[..., half_width:]
    return jnp.concatenate(
        [first_half * cosine - second * sine_part, second * cosine + first_half * sine_part],
        axis=-1,
    )


def doc_layout(doc_lengths, positions):
    doc_ends = jnp.cumsum(doc_lengths)
    passed = (positions[:, None] >= doc_ends[None, :]).astype(jnp.int32)
    document = jnp.sum(passed, axis=1)
    doc_start = jnp.sum(passed * doc_lengths[None, :], axis=1)
    return (document, positions - doc_start)


def expert_rows(rows, gate_up_weight, down_weight):
    hidden = down_weight.shape[0]
    both = jnp.dot(rows, gate_up_weight, preferred_element_type=jnp.float32)
    gate_part = both[:, :hidden]
    up_part = both[:, hidden:]
    activated = lax.optimization_barrier((jax.nn.silu(gate_part) * up_part).astype(jnp.bfloat16))
    return jnp.dot(activated, down_weight, preferred_element_type=jnp.float32).astype(jnp.bfloat16)


def per_device(
    tokens,
    query_weight,
    key_value_weight,
    out_weight,
    doc_lengths,
    expert_ids,
    router_weight,
    gate_weight,
    up_weight,
    down_weight,
):
    tok_dev, model_width = tokens.shape
    head_dim = HD
    per_group = query_weight.shape[1] // head_dim
    nx = lax.axis_size("x")
    ny = lax.axis_size("y")
    nc = lax.axis_size("c")
    xi = lax.axis_index("x")
    yi = lax.axis_index("y")
    zi = lax.axis_index("z")
    ci = lax.axis_index("c")
    shard = zi * nc + ci
    group = xi * ny + yi
    experts = router_weight.shape[1]
    own_count = tok_dev // (nx * ny)
    capacity = own_count * 3 // 4

    positions = shard * tok_dev + jnp.arange(tok_dev, dtype=jnp.int32)
    document, in_document = doc_layout(doc_lengths, positions)
    normed_in = rms_rows(tokens).astype(jnp.bfloat16)
    queries = jnp.dot(normed_in, query_weight, preferred_element_type=jnp.float32).reshape(
        tok_dev, per_group, head_dim
    )
    queries = rotate(queries, in_document).astype(jnp.bfloat16)
    half_part = jnp.dot(normed_in, key_value_weight, preferred_element_type=jnp.float32)
    rotated = rotate(half_part[:, None, :], in_document)[:, 0, :]
    holds_keys = group % 2 == 0
    mine = jnp.where(holds_keys, rotated, half_part).astype(jnp.bfloat16)
    pairs = [(i, i ^ 1) for i in range(ny)]
    partner = lax.ppermute(mine, "y", pairs)
    key_rows = jnp.where(holds_keys, mine, partner)
    values = jnp.where(holds_keys, partner, mine)
    both = jnp.stack([key_rows, values], axis=0)
    nz = lax.axis_size("z")
    core_swap = [(i, i ^ 1) for i in range(nc)]
    other_core = lax.ppermute(both, "c", core_swap)
    pair = jnp.where(ci == 0, jnp.stack([both, other_core]), jnp.stack([other_core, both]))
    ring = [pair] + [
        lax.ppermute(pair, "z", [(i, (i - k) % nz) for i in range(nz)]) for k in range(1, nz)
    ]
    gathered = jnp.stack(ring).transpose(2, 0, 1, 3, 4).reshape(2, -1, head_dim)
    key_piece = gathered[0]
    value_piece = gathered[1]
    ring_range = jnp.arange(nz, dtype=jnp.int32)
    shard_of = ((zi + ring_range) % nz)[:, None] * nc + jnp.arange(nc, dtype=jnp.int32)[None, :]
    key_places = (
        shard_of[:, :, None] * tok_dev + jnp.arange(tok_dev, dtype=jnp.int32)[None, None, :]
    ).reshape(-1)
    key_doc, unused = doc_layout(doc_lengths, key_places)
    allowed = (document[:, None] == key_doc[None, :]) & (key_places[None, :] <= positions[:, None])
    scores = (
        jnp.einsum("tqd,jd->tqj", queries, key_piece, preferred_element_type=jnp.float32)
        * head_dim ** (-0.5)
    )
    masked = jnp.where(allowed[:, None, :], scores, MASKED_SCORE)
    row_max = jnp.max(masked, axis=2)
    expo = jnp.where(allowed[:, None, :], jnp.exp(masked - row_max[..., None]), 0.0)
    denom = jnp.sum(expo, axis=2)
    weighted = jnp.einsum(
        "tqj,jd->tqd", expo.astype(jnp.bfloat16), value_piece, preferred_element_type=jnp.float32
    )
    context = (
        (weighted / denom[..., None]).astype(jnp.bfloat16).reshape(tok_dev, per_group * head_dim)
    )
    partial_value = jnp.dot(context, out_weight, preferred_element_type=jnp.float32)
    blocks = partial_value.astype(jnp.bfloat16).reshape(nx * ny, own_count, model_width)
    attention = jnp.sum(
        lax.all_to_all(blocks, ("x", "y"), split_axis=0, concat_axis=0, tiled=True).astype(
            jnp.float32
        ),
        axis=0,
    )

    own_tokens = lax.dynamic_slice_in_dim(tokens, group * own_count, own_count, 0)
    hidden_state = own_tokens.astype(jnp.float32) + attention
    normed = rms_rows(hidden_state).astype(jnp.bfloat16)
    logits = jnp.dot(normed, router_weight, preferred_element_type=jnp.float32)
    expert_range = jnp.arange(experts, dtype=jnp.int32)
    matches = expert_ids[:, :, None] == expert_range[None, None, :]
    picked = jnp.sum(jnp.where(matches, logits[:, None, :], 0.0), axis=2)
    gates = jax.nn.softmax(picked, axis=1)
    gate_cols = jnp.sum(jnp.where(matches, gates[:, :, None], 0.0), axis=1)
    names = jnp.any(matches, axis=1).astype(jnp.int32)
    slot = jnp.cumsum(names, axis=0) - names
    slot_range = jnp.arange(capacity, dtype=jnp.int32)
    hits = (slot[:, :, None] == slot_range) & (names[:, :, None] > 0)
    shift = (xi + jnp.arange(nx, dtype=jnp.int32)) % nx
    hits = jnp.take(hits, shift, axis=1)
    gate_cols = jnp.take(gate_cols, shift, axis=1)
    send = jnp.einsum(
        "rec,rd->ecd", hits.astype(jnp.bfloat16), normed, preferred_element_type=jnp.float32
    ).astype(jnp.bfloat16)

    arrived = [send[0]] + [
        lax.ppermute(send[k], "x", [(i, (i + k) % nx) for i in range(nx)]) for k in range(1, nx)
    ]
    arrived = jnp.concatenate(arrived, axis=0)
    rows = lax.all_gather(arrived, ("c", "z", "y"), axis=0, tiled=True)
    gate_up_weight = jnp.concatenate([gate_weight, up_weight], axis=1)
    line_rows = rows.shape[0] // nc
    other_rows = lax.dynamic_slice_in_dim(rows, (1 - ci) * line_rows, line_rows, 0)
    own_rows = lax.dynamic_slice_in_dim(rows, ci * line_rows, line_rows, 0)
    other_out = expert_rows(other_rows, gate_up_weight, down_weight)
    other_back = lax.ppermute(other_out, "c", core_swap)
    own_out = expert_rows(own_rows, gate_up_weight, down_weight)
    summed = (own_out.astype(jnp.float32) + other_back.astype(jnp.float32)).astype(jnp.bfloat16)

    lines = summed.reshape(-1, experts * capacity, model_width)
    summed = jnp.sum(
        lax.all_to_all(lines, ("z", "y"), split_axis=0, concat_axis=0, tiled=True).astype(
            jnp.float32
        ),
        axis=0,
    )
    summed = summed.reshape(experts, capacity, model_width).astype(jnp.bfloat16)
    returned = jnp.stack(
        [summed[0]]
        + [
            lax.ppermute(summed[k], "x", [(i, (i - k) % nx) for i in range(nx)])
            for k in range(1, nx)
        ]
    )

    weights = jnp.where(hits, gate_cols[:, :, None], 0.0)
    moe = jnp.einsum(
        "rec,ecd->rd", weights, returned.astype(jnp.float32), precision=lax.Precision.HIGHEST
    )
    return (hidden_state + moe).astype(jnp.bfloat16)


def solution(mesh):
    dp_size = mesh.shape["dp"]

    def run(*args):
        experts = args[6].shape[1]
        ex_size = mesh.shape["expert"]
        devices = np.asarray(mesh.devices).reshape(
            dp_size // CORES, CORES, experts, ex_size // experts
        )
        fine = Mesh(devices, ("z", "c", "x", "y"))
        tok = ("z", "c")
        grp = ("x", "y")
        placed = (
            P(tok, None),
            P(None, grp),
            P(None, grp),
            P(grp, None),
            P(),
            P(tok + grp, None),
            P(),
            P(None, grp + tok),
            P(None, grp + tok),
            P(grp + tok, None),
        )
        body = jax.shard_map(
            per_device, mesh=fine, in_specs=placed, out_specs=P(tok + grp, None), check_vma=False
        )
        return body(*args)

    return run
```

```python
import jax
import jax.numpy as jnp
import numpy as np
from jax import lax
from jax.sharding import Mesh
from jax.sharding import PartitionSpec as P

HD = 128
CORES = 2

EPSILON = 1e-05
ROPE_BASE = 1000000.0
MASKED_SCORE = -1e30


def rms_rows(matrix):
    matrix = matrix.astype(jnp.float32)
    return matrix * lax.rsqrt(jnp.mean(matrix * matrix, axis=-1, keepdims=True) + EPSILON)


def rotate(vectors, positions):
    half_width = vectors.shape[-1] // 2
    frequency = ROPE_BASE ** (-jnp.arange(half_width, dtype=jnp.float32) * 2.0 / vectors.shape[-1])
    angles = positions.astype(jnp.float32)[:, None] * frequency[None, :]
    cosine = jnp.cos(angles)[:, None, :]
    sine_part = jnp.sin(angles)[:, None, :]
    first_half = vectors[..., :half_width]
    second = vectors[..., half_width:]
    return jnp.concatenate(
        [first_half * cosine - second * sine_part, second * cosine + first_half * sine_part],
        axis=-1,
    )


def doc_layout(doc_lengths, positions):
    doc_ends = jnp.cumsum(doc_lengths)
    passed = (positions[:, None] >= doc_ends[None, :]).astype(jnp.int32)
    document = jnp.sum(passed, axis=1)
    doc_start = jnp.sum(passed * doc_lengths[None, :], axis=1)
    return (document, positions - doc_start)


def expert_rows(rows, gate_up_weight, down_weight):
    hidden = down_weight.shape[0]
    both = jnp.dot(rows, gate_up_weight, preferred_element_type=jnp.float32)
    gate_part = both[:, :hidden]
    up_part = both[:, hidden:]
    activated = lax.optimization_barrier((jax.nn.silu(gate_part) * up_part).astype(jnp.bfloat16))
    return jnp.dot(activated, down_weight, preferred_element_type=jnp.float32).astype(jnp.bfloat16)


def per_device(
    tokens,
    query_weight,
    key_value_weight,
    out_weight,
    doc_lengths,
    expert_ids,
    router_weight,
    gate_weight,
    up_weight,
    down_weight,
):
    tok_dev, model_width = tokens.shape
    head_dim = HD
    per_group = query_weight.shape[1] // head_dim
    nx = lax.axis_size("x")
    ny = lax.axis_size("y")
    nc = lax.axis_size("c")
    xi = lax.axis_index("x")
    yi = lax.axis_index("y")
    zi = lax.axis_index("z")
    ci = lax.axis_index("c")
    shard = zi * nc + ci
    group = xi * ny + yi
    experts = router_weight.shape[1]
    own_count = tok_dev // (nx * ny)
    capacity = own_count * 3 // 4

    positions = shard * tok_dev + jnp.arange(tok_dev, dtype=jnp.int32)
    document, in_document = doc_layout(doc_lengths, positions)
    normed_in = rms_rows(tokens).astype(jnp.bfloat16)
    queries = jnp.dot(normed_in, query_weight, preferred_element_type=jnp.float32).reshape(
        tok_dev, per_group, head_dim
    )
    queries = rotate(queries, in_document).astype(jnp.bfloat16)
    half_part = jnp.dot(normed_in, key_value_weight, preferred_element_type=jnp.float32)
    rotated = rotate(half_part[:, None, :], in_document)[:, 0, :]
    holds_keys = group % 2 == 0
    mine = jnp.where(holds_keys, rotated, half_part).astype(jnp.bfloat16)
    pairs = [(i, i ^ 1) for i in range(ny)]
    partner = lax.ppermute(mine, "y", pairs)
    key_rows = jnp.where(holds_keys, mine, partner)
    values = jnp.where(holds_keys, partner, mine)
    both = jnp.stack([key_rows, values], axis=0)
    nz = lax.axis_size("z")
    core_swap = [(i, i ^ 1) for i in range(nc)]
    other_core = lax.ppermute(both, "c", core_swap)
    pair = jnp.stack([both, other_core])
    ring = [pair] + [
        lax.ppermute(pair, "z", [(i, (i - k) % nz) for i in range(nz)]) for k in range(1, nz)
    ]
    gathered = jnp.stack(ring).transpose(2, 0, 1, 3, 4).reshape(2, -1, head_dim)
    key_piece = gathered[0]
    value_piece = gathered[1]
    ring_range = jnp.arange(nz, dtype=jnp.int32)
    core_order = (ci + jnp.arange(nc, dtype=jnp.int32)) % nc
    shard_of = ((zi + ring_range) % nz)[:, None] * nc + core_order[None, :]
    key_places = (
        shard_of[:, :, None] * tok_dev + jnp.arange(tok_dev, dtype=jnp.int32)[None, None, :]
    ).reshape(-1)
    key_doc, unused = doc_layout(doc_lengths, key_places)
    allowed = (document[:, None] == key_doc[None, :]) & (key_places[None, :] <= positions[:, None])
    scores = (
        jnp.einsum("tqd,jd->tqj", queries, key_piece, preferred_element_type=jnp.float32)
        * head_dim ** (-0.5)
    )
    masked = jnp.where(allowed[:, None, :], scores, MASKED_SCORE)
    row_max = jnp.max(masked, axis=2)
    expo = jnp.where(allowed[:, None, :], jnp.exp(masked - row_max[..., None]), 0.0)
    denom = jnp.sum(expo, axis=2)
    weighted = jnp.einsum(
        "tqj,jd->tqd", expo.astype(jnp.bfloat16), value_piece, preferred_element_type=jnp.float32
    )
    context = (
        (weighted / denom[..., None]).astype(jnp.bfloat16).reshape(tok_dev, per_group * head_dim)
    )
    partial_value = jnp.dot(context, out_weight, preferred_element_type=jnp.float32)
    blocks = partial_value.astype(jnp.bfloat16).reshape(nx * ny, own_count, model_width)
    attention = jnp.sum(
        lax.all_to_all(blocks, ("x", "y"), split_axis=0, concat_axis=0, tiled=True).astype(
            jnp.float32
        ),
        axis=0,
    )

    own_tokens = lax.dynamic_slice_in_dim(tokens, group * own_count, own_count, 0)
    hidden_state = own_tokens.astype(jnp.float32) + attention
    normed = rms_rows(hidden_state).astype(jnp.bfloat16)
    logits = jnp.dot(normed, router_weight, preferred_element_type=jnp.float32)
    expert_range = jnp.arange(experts, dtype=jnp.int32)
    matches = expert_ids[:, :, None] == expert_range[None, None, :]
    picked = jnp.sum(jnp.where(matches, logits[:, None, :], 0.0), axis=2)
    gates = jax.nn.softmax(picked, axis=1)
    gate_cols = jnp.sum(jnp.where(matches, gates[:, :, None], 0.0), axis=1)
    names = jnp.any(matches, axis=1).astype(jnp.int32)
    slot = jnp.cumsum(names, axis=0) - names
    slot_range = jnp.arange(capacity, dtype=jnp.int32)
    hits = (slot[:, :, None] == slot_range) & (names[:, :, None] > 0)
    shift = (xi + jnp.arange(nx, dtype=jnp.int32)) % nx
    hits = jnp.take(hits, shift, axis=1)
    gate_cols = jnp.take(gate_cols, shift, axis=1)
    send = jnp.einsum(
        "rec,rd->ecd", hits.astype(jnp.bfloat16), normed, preferred_element_type=jnp.float32
    ).astype(jnp.bfloat16)

    arrived = [send[0]] + [
        lax.ppermute(send[k], "x", [(i, (i + k) % nx) for i in range(nx)]) for k in range(1, nx)
    ]
    arrived = jnp.concatenate(arrived, axis=0)
    rows = lax.all_gather(arrived, ("c", "y", "z"), axis=0, tiled=True)
    gate_up_weight = jnp.concatenate([gate_weight, up_weight], axis=1)
    line_rows = rows.shape[0] // nc
    other_rows = lax.dynamic_slice_in_dim(rows, (1 - ci) * line_rows, line_rows, 0)
    own_rows = lax.dynamic_slice_in_dim(rows, ci * line_rows, line_rows, 0)
    other_out = expert_rows(other_rows, gate_up_weight, down_weight)
    other_back = lax.ppermute(other_out, "c", core_swap)
    own_out = expert_rows(own_rows, gate_up_weight, down_weight)
    summed = (own_out.astype(jnp.float32) + other_back.astype(jnp.float32)).astype(jnp.bfloat16)

    lines = summed.reshape(-1, experts * capacity, model_width)
    summed = jnp.sum(
        lax.all_to_all(lines, ("y", "z"), split_axis=0, concat_axis=0, tiled=True).astype(
            jnp.float32
        ),
        axis=0,
    )
    summed = summed.reshape(experts, capacity, model_width).astype(jnp.bfloat16)
    returned = jnp.stack(
        [summed[0]]
        + [
            lax.ppermute(summed[k], "x", [(i, (i - k) % nx) for i in range(nx)])
            for k in range(1, nx)
        ]
    )

    weights = jnp.where(hits, gate_cols[:, :, None], 0.0)
    moe = jnp.einsum(
        "rec,ecd->rd", weights, returned.astype(jnp.float32), precision=lax.Precision.HIGHEST
    )
    return (hidden_state + moe).astype(jnp.bfloat16)


def solution(mesh):
    dp_size = mesh.shape["dp"]

    def run(*args):
        experts = args[6].shape[1]
        ex_size = mesh.shape["expert"]
        devices = np.asarray(mesh.devices).reshape(
            dp_size // CORES, CORES, experts, ex_size // experts
        )
        fine = Mesh(devices, ("z", "c", "x", "y"))
        tok = ("z", "c")
        grp = ("x", "y")
        placed = (
            P(tok, None),
            P(None, grp),
            P(None, grp),
            P(grp, None),
            P(),
            P(tok + grp, None),
            P(),
            P(None, grp + tok),
            P(None, grp + tok),
            P(grp + tok, None),
        )
        body = jax.shard_map(
            per_device, mesh=fine, in_specs=placed, out_specs=P(tok + grp, None), check_vma=False
        )
        return body(*args)

    return run
```

```python
import jax
import jax.numpy as jnp
import numpy as np
from jax import lax
from jax.sharding import Mesh
from jax.sharding import PartitionSpec as P

HD = 128
CORES = 2

EPSILON = 1e-05
ROPE_BASE = 1000000.0
MASKED_SCORE = -1e30


def rms_rows(matrix):
    matrix = matrix.astype(jnp.float32)
    return matrix * lax.rsqrt(jnp.mean(matrix * matrix, axis=-1, keepdims=True) + EPSILON)


def rotate(vectors, positions):
    half_width = vectors.shape[-1] // 2
    frequency = ROPE_BASE ** (-jnp.arange(half_width, dtype=jnp.float32) * 2.0 / vectors.shape[-1])
    angles = positions.astype(jnp.float32)[:, None] * frequency[None, :]
    cosine = jnp.cos(angles)[:, None, :]
    sine_part = jnp.sin(angles)[:, None, :]
    first_half = vectors[..., :half_width]
    second = vectors[..., half_width:]
    return jnp.concatenate(
        [first_half * cosine - second * sine_part, second * cosine + first_half * sine_part],
        axis=-1,
    )


def doc_layout(doc_lengths, positions):
    doc_ends = jnp.cumsum(doc_lengths)
    passed = (positions[:, None] >= doc_ends[None, :]).astype(jnp.int32)
    document = jnp.sum(passed, axis=1)
    doc_start = jnp.sum(passed * doc_lengths[None, :], axis=1)
    return (document, positions - doc_start)


def expert_rows(rows, gate_up_weight, down_weight):
    hidden = down_weight.shape[0]
    both = jnp.dot(rows, gate_up_weight, preferred_element_type=jnp.float32)
    gate_part = both[:, :hidden]
    up_part = both[:, hidden:]
    activated = lax.optimization_barrier((jax.nn.silu(gate_part) * up_part).astype(jnp.bfloat16))
    return jnp.dot(activated, down_weight, preferred_element_type=jnp.float32).astype(jnp.bfloat16)


def per_device(
    tokens,
    query_weight,
    key_value_weight,
    out_weight,
    doc_lengths,
    expert_ids,
    router_weight,
    gate_weight,
    up_weight,
    down_weight,
):
    tok_dev, model_width = tokens.shape
    head_dim = HD
    per_group = query_weight.shape[1] // head_dim
    nx = lax.axis_size("x")
    ny = lax.axis_size("y")
    nc = lax.axis_size("c")
    xi = lax.axis_index("x")
    yi = lax.axis_index("y")
    zi = lax.axis_index("z")
    ci = lax.axis_index("c")
    shard = zi * nc + ci
    group = xi * ny + yi
    experts = router_weight.shape[1]
    own_count = tok_dev // (nx * ny)
    capacity = own_count * 3 // 4

    positions = shard * tok_dev + jnp.arange(tok_dev, dtype=jnp.int32)
    document, in_document = doc_layout(doc_lengths, positions)
    normed_in = rms_rows(tokens).astype(jnp.bfloat16)
    queries = jnp.dot(normed_in, query_weight, preferred_element_type=jnp.float32).reshape(
        tok_dev, per_group, head_dim
    )
    queries = rotate(queries, in_document).astype(jnp.bfloat16)
    half_part = jnp.dot(normed_in, key_value_weight, preferred_element_type=jnp.float32)
    rotated = rotate(half_part[:, None, :], in_document)[:, 0, :]
    holds_keys = group % 2 == 0
    mine = jnp.where(holds_keys, rotated, half_part).astype(jnp.bfloat16)
    pairs = [(i, i ^ 1) for i in range(ny)]
    partner = lax.ppermute(mine, "y", pairs)
    key_rows = jnp.where(holds_keys, mine, partner)
    values = jnp.where(holds_keys, partner, mine)
    both = jnp.stack([key_rows, values], axis=0)
    nz = lax.axis_size("z")
    core_swap = [(i, i ^ 1) for i in range(nc)]
    other_core = lax.ppermute(both, "c", core_swap)
    pair = jnp.where(ci == 0, jnp.stack([both, other_core]), jnp.stack([other_core, both]))
    ring = [pair] + [
        lax.ppermute(pair, "z", [(i, (i - k) % nz) for i in range(nz)]) for k in range(1, nz)
    ]
    gathered = jnp.stack(ring).transpose(2, 0, 1, 3, 4).reshape(2, -1, head_dim)
    key_piece = gathered[0]
    value_piece = gathered[1]
    ring_range = jnp.arange(nz, dtype=jnp.int32)
    shard_of = ((zi + ring_range) % nz)[:, None] * nc + jnp.arange(nc, dtype=jnp.int32)[None, :]
    key_places = (
        shard_of[:, :, None] * tok_dev + jnp.arange(tok_dev, dtype=jnp.int32)[None, None, :]
    ).reshape(-1)
    key_doc, unused = doc_layout(doc_lengths, key_places)
    allowed = (document[:, None] == key_doc[None, :]) & (key_places[None, :] <= positions[:, None])
    scores = (
        jnp.einsum("tqd,jd->tqj", queries, key_piece, preferred_element_type=jnp.float32)
        * head_dim ** (-0.5)
    )
    masked = jnp.where(allowed[:, None, :], scores, MASKED_SCORE)
    row_max = jnp.max(masked, axis=2)
    expo = jnp.where(allowed[:, None, :], jnp.exp(masked - row_max[..., None]), 0.0)
    denom = jnp.sum(expo, axis=2)
    weighted = jnp.einsum(
        "tqj,jd->tqd", expo.astype(jnp.bfloat16), value_piece, preferred_element_type=jnp.float32
    )
    context = (
        (weighted / denom[..., None]).astype(jnp.bfloat16).reshape(tok_dev, per_group * head_dim)
    )
    partial_value = jnp.dot(context, out_weight, preferred_element_type=jnp.float32)
    blocks = partial_value.astype(jnp.bfloat16).reshape(nx * ny, own_count, model_width)
    attention = jnp.sum(
        lax.all_to_all(blocks, ("x", "y"), split_axis=0, concat_axis=0, tiled=True).astype(
            jnp.float32
        ),
        axis=0,
    )

    own_tokens = lax.dynamic_slice_in_dim(tokens, group * own_count, own_count, 0)
    hidden_state = own_tokens.astype(jnp.float32) + attention
    normed = rms_rows(hidden_state).astype(jnp.bfloat16)
    logits = jnp.dot(normed, router_weight, preferred_element_type=jnp.float32)
    expert_range = jnp.arange(experts, dtype=jnp.int32)
    matches = expert_ids[:, :, None] == expert_range[None, None, :]
    picked = jnp.sum(jnp.where(matches, logits[:, None, :], 0.0), axis=2)
    gates = jax.nn.softmax(picked, axis=1)
    gate_cols = jnp.sum(jnp.where(matches, gates[:, :, None], 0.0), axis=1)
    names = jnp.any(matches, axis=1).astype(jnp.int32)
    slot = jnp.cumsum(names, axis=0) - names
    slot_range = jnp.arange(capacity, dtype=jnp.int32)
    hits = (slot[:, :, None] == slot_range) & (names[:, :, None] > 0)
    shift = (xi + jnp.arange(nx, dtype=jnp.int32)) % nx
    hits = jnp.take(hits, shift, axis=1)
    gate_cols = jnp.take(gate_cols, shift, axis=1)
    send = jnp.einsum(
        "rec,rd->ecd", hits.astype(jnp.bfloat16), normed, preferred_element_type=jnp.float32
    ).astype(jnp.bfloat16)

    arrived = [send[0]] + [
        lax.ppermute(send[k], "x", [(i, (i + k) % nx) for i in range(nx)]) for k in range(1, nx)
    ]
    arrived = jnp.concatenate(arrived, axis=0)
    rows = lax.all_gather(arrived, ("c", "y", "z"), axis=0, tiled=True)
    gate_up_weight = jnp.concatenate([gate_weight, up_weight], axis=1)
    line_rows = rows.shape[0] // nc
    other_rows = lax.dynamic_slice_in_dim(rows, (1 - ci) * line_rows, line_rows, 0)
    own_rows = lax.dynamic_slice_in_dim(rows, ci * line_rows, line_rows, 0)
    other_out = expert_rows(other_rows, gate_up_weight, down_weight)
    other_back = lax.ppermute(other_out, "c", core_swap)
    own_out = expert_rows(own_rows, gate_up_weight, down_weight)
    summed = (own_out.astype(jnp.float32) + other_back.astype(jnp.float32)).astype(jnp.bfloat16)

    lines = summed.reshape(-1, experts * capacity, model_width)
    summed = jnp.sum(
        lax.all_to_all(lines, ("y", "z"), split_axis=0, concat_axis=0, tiled=True).astype(
            jnp.float32
        ),
        axis=0,
    )
    summed = summed.reshape(experts, capacity, model_width).astype(jnp.bfloat16)
    returned = jnp.stack(
        [summed[0]]
        + [
            lax.ppermute(summed[k], "x", [(i, (i - k) % nx) for i in range(nx)])
            for k in range(1, nx)
        ]
    )

    chosen = jnp.take(matches, shift, axis=2)[:, :, :, None] & hits[:, None, :, :]
    picked_rows = jnp.einsum(
        "rkec,ecd->rkd",
        chosen.astype(jnp.bfloat16),
        returned,
        preferred_element_type=jnp.float32,
    )
    moe = jnp.sum(gates[:, :, None] * picked_rows, axis=1)
    return (hidden_state + moe).astype(jnp.bfloat16)


def solution(mesh):
    dp_size = mesh.shape["dp"]

    def run(*args):
        experts = args[6].shape[1]
        ex_size = mesh.shape["expert"]
        devices = np.asarray(mesh.devices).reshape(
            dp_size // CORES, CORES, experts, ex_size // experts
        )
        fine = Mesh(devices, ("z", "c", "x", "y"))
        tok = ("z", "c")
        grp = ("x", "y")
        placed = (
            P(tok, None),
            P(None, grp),
            P(None, grp),
            P(grp, None),
            P(),
            P(tok + grp, None),
            P(),
            P(None, grp + tok),
            P(None, grp + tok),
            P(grp + tok, None),
        )
        body = jax.shard_map(
            per_device, mesh=fine, in_specs=placed, out_specs=P(tok + grp, None), check_vma=False
        )
        return body(*args)

    return run
```

```python
import jax
import jax.numpy as jnp
import numpy as np
from jax import lax
from jax.sharding import Mesh
from jax.sharding import PartitionSpec as P

HD = 128
CORES = 2

EPSILON = 1e-05
ROPE_BASE = 1000000.0
MASKED_SCORE = -1e30


def rms_rows(matrix):
    matrix = matrix.astype(jnp.float32)
    return matrix * lax.rsqrt(jnp.mean(matrix * matrix, axis=-1, keepdims=True) + EPSILON)


def rotate(vectors, positions):
    half_width = vectors.shape[-1] // 2
    frequency = ROPE_BASE ** (-jnp.arange(half_width, dtype=jnp.float32) * 2.0 / vectors.shape[-1])
    angles = positions.astype(jnp.float32)[:, None] * frequency[None, :]
    cosine = jnp.cos(angles)[:, None, :]
    sine_part = jnp.sin(angles)[:, None, :]
    first_half = vectors[..., :half_width]
    second = vectors[..., half_width:]
    return jnp.concatenate(
        [first_half * cosine - second * sine_part, second * cosine + first_half * sine_part],
        axis=-1,
    )


def doc_layout(doc_lengths, positions):
    doc_ends = jnp.cumsum(doc_lengths)
    passed = (positions[:, None] >= doc_ends[None, :]).astype(jnp.int32)
    document = jnp.sum(passed, axis=1)
    doc_start = jnp.sum(passed * doc_lengths[None, :], axis=1)
    return (document, positions - doc_start)


def expert_rows(rows, gate_up_weight, down_weight):
    hidden = down_weight.shape[0]
    both = jnp.dot(rows, gate_up_weight, preferred_element_type=jnp.float32)
    gate_part = both[:, :hidden]
    up_part = both[:, hidden:]
    activated = lax.optimization_barrier((jax.nn.silu(gate_part) * up_part).astype(jnp.bfloat16))
    return jnp.dot(activated, down_weight, preferred_element_type=jnp.float32).astype(jnp.bfloat16)


def per_device(
    tokens,
    query_weight,
    key_value_weight,
    out_weight,
    doc_lengths,
    expert_ids,
    router_weight,
    gate_weight,
    up_weight,
    down_weight,
):
    tok_dev, model_width = tokens.shape
    head_dim = HD
    per_group = query_weight.shape[1] // head_dim
    nx = lax.axis_size("x")
    ny = lax.axis_size("y")
    nc = lax.axis_size("c")
    xi = lax.axis_index("x")
    yi = lax.axis_index("y")
    zi = lax.axis_index("z")
    ci = lax.axis_index("c")
    shard = zi * nc + ci
    group = xi * ny + yi
    experts = router_weight.shape[1]
    own_count = tok_dev // (nx * ny)
    capacity = own_count * 3 // 4

    positions = shard * tok_dev + jnp.arange(tok_dev, dtype=jnp.int32)
    document, in_document = doc_layout(doc_lengths, positions)
    normed_in = rms_rows(tokens).astype(jnp.bfloat16)
    half_part = jnp.dot(normed_in, key_value_weight, preferred_element_type=jnp.float32)
    rotated = rotate(half_part[:, None, :], in_document)[:, 0, :]
    holds_keys = group % 2 == 0
    mine = jnp.where(holds_keys, rotated, half_part).astype(jnp.bfloat16)
    pairs = [(i, i ^ 1) for i in range(ny)]
    partner = lax.ppermute(mine, "y", pairs)
    key_rows = jnp.where(holds_keys, mine, partner)
    values = jnp.where(holds_keys, partner, mine)
    both = jnp.stack([key_rows, values], axis=0)
    nz = lax.axis_size("z")
    core_swap = [(i, i ^ 1) for i in range(nc)]
    other_core = lax.ppermute(both, "c", core_swap)
    pair = jnp.where(ci == 0, jnp.stack([both, other_core]), jnp.stack([other_core, both]))
    ring = [pair] + [
        lax.ppermute(pair, "z", [(i, (i - k) % nz) for i in range(nz)]) for k in range(1, nz)
    ]
    query_in, unused = lax.optimization_barrier((normed_in, pair))
    queries = jnp.dot(query_in, query_weight, preferred_element_type=jnp.float32).reshape(
        tok_dev, per_group, head_dim
    )
    queries = rotate(queries, in_document).astype(jnp.bfloat16)
    gathered = jnp.stack(ring).transpose(2, 0, 1, 3, 4).reshape(2, -1, head_dim)
    key_piece = gathered[0]
    value_piece = gathered[1]
    ring_range = jnp.arange(nz, dtype=jnp.int32)
    shard_of = ((zi + ring_range) % nz)[:, None] * nc + jnp.arange(nc, dtype=jnp.int32)[None, :]
    key_places = (
        shard_of[:, :, None] * tok_dev + jnp.arange(tok_dev, dtype=jnp.int32)[None, None, :]
    ).reshape(-1)
    key_doc, unused = doc_layout(doc_lengths, key_places)
    allowed = (document[:, None] == key_doc[None, :]) & (key_places[None, :] <= positions[:, None])
    scores = (
        jnp.einsum("tqd,jd->tqj", queries, key_piece, preferred_element_type=jnp.float32)
        * head_dim ** (-0.5)
    )
    masked = jnp.where(allowed[:, None, :], scores, MASKED_SCORE)
    row_max = jnp.max(masked, axis=2)
    expo = jnp.where(allowed[:, None, :], jnp.exp(masked - row_max[..., None]), 0.0)
    denom = jnp.sum(expo, axis=2)
    weighted = jnp.einsum(
        "tqj,jd->tqd", expo.astype(jnp.bfloat16), value_piece, preferred_element_type=jnp.float32
    )
    context = (
        (weighted / denom[..., None]).astype(jnp.bfloat16).reshape(tok_dev, per_group * head_dim)
    )
    partial_value = jnp.dot(context, out_weight, preferred_element_type=jnp.float32)
    blocks = partial_value.astype(jnp.bfloat16).reshape(nx * ny, own_count, model_width)
    attention = jnp.sum(
        lax.all_to_all(blocks, ("x", "y"), split_axis=0, concat_axis=0, tiled=True).astype(
            jnp.float32
        ),
        axis=0,
    )

    own_tokens = lax.dynamic_slice_in_dim(tokens, group * own_count, own_count, 0)
    hidden_state = own_tokens.astype(jnp.float32) + attention
    normed = rms_rows(hidden_state).astype(jnp.bfloat16)
    logits = jnp.dot(normed, router_weight, preferred_element_type=jnp.float32)
    expert_range = jnp.arange(experts, dtype=jnp.int32)
    matches = expert_ids[:, :, None] == expert_range[None, None, :]
    picked = jnp.sum(jnp.where(matches, logits[:, None, :], 0.0), axis=2)
    gates = jax.nn.softmax(picked, axis=1)
    gate_cols = jnp.sum(jnp.where(matches, gates[:, :, None], 0.0), axis=1)
    names = jnp.any(matches, axis=1).astype(jnp.int32)
    slot = jnp.cumsum(names, axis=0) - names
    slot_range = jnp.arange(capacity, dtype=jnp.int32)
    hits = (slot[:, :, None] == slot_range) & (names[:, :, None] > 0)
    shift = (xi + jnp.arange(nx, dtype=jnp.int32)) % nx
    hits = jnp.take(hits, shift, axis=1)
    gate_cols = jnp.take(gate_cols, shift, axis=1)
    send = jnp.einsum(
        "rec,rd->ecd", hits.astype(jnp.bfloat16), normed, preferred_element_type=jnp.float32
    ).astype(jnp.bfloat16)

    arrived = [send[0]] + [
        lax.ppermute(send[k], "x", [(i, (i + k) % nx) for i in range(nx)]) for k in range(1, nx)
    ]
    arrived = jnp.concatenate(arrived, axis=0)
    rows = lax.all_gather(arrived, ("c", "y", "z"), axis=0, tiled=True)
    gate_up_weight = jnp.concatenate([gate_weight, up_weight], axis=1)
    line_rows = rows.shape[0] // nc
    other_rows = lax.dynamic_slice_in_dim(rows, (1 - ci) * line_rows, line_rows, 0)
    own_rows = lax.dynamic_slice_in_dim(rows, ci * line_rows, line_rows, 0)
    other_out = expert_rows(other_rows, gate_up_weight, down_weight)
    other_back = lax.ppermute(other_out, "c", core_swap)
    own_out = expert_rows(own_rows, gate_up_weight, down_weight)
    summed = (own_out.astype(jnp.float32) + other_back.astype(jnp.float32)).astype(jnp.bfloat16)

    lines = summed.reshape(-1, experts * capacity, model_width)
    summed = jnp.sum(
        lax.all_to_all(lines, ("y", "z"), split_axis=0, concat_axis=0, tiled=True).astype(
            jnp.float32
        ),
        axis=0,
    )
    summed = summed.reshape(experts, capacity, model_width).astype(jnp.bfloat16)
    returned = jnp.stack(
        [summed[0]]
        + [
            lax.ppermute(summed[k], "x", [(i, (i - k) % nx) for i in range(nx)])
            for k in range(1, nx)
        ]
    )

    weights = jnp.where(hits, gate_cols[:, :, None], 0.0)
    moe = jnp.einsum(
        "rec,ecd->rd", weights, returned.astype(jnp.float32), precision=lax.Precision.HIGHEST
    )
    return (hidden_state + moe).astype(jnp.bfloat16)


def solution(mesh):
    dp_size = mesh.shape["dp"]

    def run(*args):
        experts = args[6].shape[1]
        ex_size = mesh.shape["expert"]
        devices = np.asarray(mesh.devices).reshape(
            dp_size // CORES, CORES, experts, ex_size // experts
        )
        fine = Mesh(devices, ("z", "c", "x", "y"))
        tok = ("z", "c")
        grp = ("x", "y")
        placed = (
            P(tok, None),
            P(None, grp),
            P(None, grp),
            P(grp, None),
            P(),
            P(tok + grp, None),
            P(),
            P(None, grp + tok),
            P(None, grp + tok),
            P(grp + tok, None),
        )
        body = jax.shard_map(
            per_device, mesh=fine, in_specs=placed, out_specs=P(tok + grp, None), check_vma=False
        )
        return body(*args)

    return run
```

```python
import jax
import jax.numpy as jnp
import numpy as np
from jax import lax
from jax.sharding import Mesh
from jax.sharding import PartitionSpec as P

HD = 128
CORES = 2

EPSILON = 1e-05
ROPE_BASE = 1000000.0
MASKED_SCORE = -1e30


def rms_rows(matrix):
    matrix = matrix.astype(jnp.float32)
    return matrix * lax.rsqrt(jnp.mean(matrix * matrix, axis=-1, keepdims=True) + EPSILON)


def rotate(vectors, positions):
    half_width = vectors.shape[-1] // 2
    frequency = ROPE_BASE ** (-jnp.arange(half_width, dtype=jnp.float32) * 2.0 / vectors.shape[-1])
    angles = positions.astype(jnp.float32)[:, None] * frequency[None, :]
    cosine = jnp.cos(angles)[:, None, :]
    sine_part = jnp.sin(angles)[:, None, :]
    first_half = vectors[..., :half_width]
    second = vectors[..., half_width:]
    return jnp.concatenate(
        [first_half * cosine - second * sine_part, second * cosine + first_half * sine_part],
        axis=-1,
    )


def doc_layout(doc_lengths, positions):
    doc_ends = jnp.cumsum(doc_lengths)
    passed = (positions[:, None] >= doc_ends[None, :]).astype(jnp.int32)
    document = jnp.sum(passed, axis=1)
    doc_start = jnp.sum(passed * doc_lengths[None, :], axis=1)
    return (document, positions - doc_start)


def expert_rows(rows, gate_up_weight, down_weight):
    hidden = down_weight.shape[0]
    both = jnp.dot(rows, gate_up_weight, preferred_element_type=jnp.float32)
    gate_part = both[:, :hidden]
    up_part = both[:, hidden:]
    activated = lax.optimization_barrier((jax.nn.silu(gate_part) * up_part).astype(jnp.bfloat16))
    return jnp.dot(activated, down_weight, preferred_element_type=jnp.float32).astype(jnp.bfloat16)


def per_device(
    tokens,
    query_weight,
    key_value_weight,
    out_weight,
    doc_lengths,
    expert_ids,
    router_weight,
    gate_weight,
    up_weight,
    down_weight,
):
    tok_dev, model_width = tokens.shape
    head_dim = HD
    per_group = query_weight.shape[1] // head_dim
    nx = lax.axis_size("x")
    ny = lax.axis_size("y")
    nc = lax.axis_size("c")
    xi = lax.axis_index("x")
    yi = lax.axis_index("y")
    zi = lax.axis_index("z")
    ci = lax.axis_index("c")
    shard = zi * nc + ci
    group = xi * ny + yi
    experts = router_weight.shape[1]
    own_count = tok_dev // (nx * ny)
    capacity = own_count * 3 // 4

    positions = shard * tok_dev + jnp.arange(tok_dev, dtype=jnp.int32)
    document, in_document = doc_layout(doc_lengths, positions)
    normed_in = rms_rows(tokens).astype(jnp.bfloat16)
    half_part = jnp.dot(normed_in, key_value_weight, preferred_element_type=jnp.float32)
    rotated = rotate(half_part[:, None, :], in_document)[:, 0, :]
    holds_keys = group % 2 == 0
    mine = jnp.where(holds_keys, rotated, half_part).astype(jnp.bfloat16)
    pairs = [(i, i ^ 1) for i in range(ny)]
    partner = lax.ppermute(mine, "y", pairs)
    key_rows = jnp.where(holds_keys, mine, partner)
    values = jnp.where(holds_keys, partner, mine)
    both = jnp.stack([key_rows, values], axis=0)
    nz = lax.axis_size("z")
    core_swap = [(i, i ^ 1) for i in range(nc)]
    other_core = lax.ppermute(both, "c", core_swap)
    pair = jnp.where(ci == 0, jnp.stack([both, other_core]), jnp.stack([other_core, both]))
    ring = [pair] + [
        lax.ppermute(pair, "z", [(i, (i - k) % nz) for i in range(nz)]) for k in range(1, nz)
    ]
    query_in, unused = lax.optimization_barrier((normed_in, pair))
    first_head = jnp.dot(
        normed_in, query_weight[:, :head_dim], preferred_element_type=jnp.float32
    )
    other_heads = jnp.dot(
        query_in, query_weight[:, head_dim:], preferred_element_type=jnp.float32
    )
    queries = jnp.concatenate([first_head, other_heads], axis=1).reshape(
        tok_dev, per_group, head_dim
    )
    queries = rotate(queries, in_document).astype(jnp.bfloat16)
    gathered = jnp.stack(ring).transpose(2, 0, 1, 3, 4).reshape(2, -1, head_dim)
    key_piece = gathered[0]
    value_piece = gathered[1]
    ring_range = jnp.arange(nz, dtype=jnp.int32)
    shard_of = ((zi + ring_range) % nz)[:, None] * nc + jnp.arange(nc, dtype=jnp.int32)[None, :]
    key_places = (
        shard_of[:, :, None] * tok_dev + jnp.arange(tok_dev, dtype=jnp.int32)[None, None, :]
    ).reshape(-1)
    key_doc, unused = doc_layout(doc_lengths, key_places)
    allowed = (document[:, None] == key_doc[None, :]) & (key_places[None, :] <= positions[:, None])
    scores = (
        jnp.einsum("tqd,jd->tqj", queries, key_piece, preferred_element_type=jnp.float32)
        * head_dim ** (-0.5)
    )
    masked = jnp.where(allowed[:, None, :], scores, MASKED_SCORE)
    row_max = jnp.max(masked, axis=2)
    expo = jnp.where(allowed[:, None, :], jnp.exp(masked - row_max[..., None]), 0.0)
    denom = jnp.sum(expo, axis=2)
    weighted = jnp.einsum(
        "tqj,jd->tqd", expo.astype(jnp.bfloat16), value_piece, preferred_element_type=jnp.float32
    )
    context = (
        (weighted / denom[..., None]).astype(jnp.bfloat16).reshape(tok_dev, per_group * head_dim)
    )
    partial_value = jnp.dot(context, out_weight, preferred_element_type=jnp.float32)
    blocks = partial_value.astype(jnp.bfloat16).reshape(nx * ny, own_count, model_width)
    attention = jnp.sum(
        lax.all_to_all(blocks, ("x", "y"), split_axis=0, concat_axis=0, tiled=True).astype(
            jnp.float32
        ),
        axis=0,
    )

    own_tokens = lax.dynamic_slice_in_dim(tokens, group * own_count, own_count, 0)
    hidden_state = own_tokens.astype(jnp.float32) + attention
    normed = rms_rows(hidden_state).astype(jnp.bfloat16)
    logits = jnp.dot(normed, router_weight, preferred_element_type=jnp.float32)
    expert_range = jnp.arange(experts, dtype=jnp.int32)
    matches = expert_ids[:, :, None] == expert_range[None, None, :]
    picked = jnp.sum(jnp.where(matches, logits[:, None, :], 0.0), axis=2)
    gates = jax.nn.softmax(picked, axis=1)
    gate_cols = jnp.sum(jnp.where(matches, gates[:, :, None], 0.0), axis=1)
    names = jnp.any(matches, axis=1).astype(jnp.int32)
    slot = jnp.cumsum(names, axis=0) - names
    slot_range = jnp.arange(capacity, dtype=jnp.int32)
    hits = (slot[:, :, None] == slot_range) & (names[:, :, None] > 0)
    shift = (xi + jnp.arange(nx, dtype=jnp.int32)) % nx
    hits = jnp.take(hits, shift, axis=1)
    gate_cols = jnp.take(gate_cols, shift, axis=1)
    send = jnp.einsum(
        "rec,rd->ecd", hits.astype(jnp.bfloat16), normed, preferred_element_type=jnp.float32
    ).astype(jnp.bfloat16)

    arrived = [send[0]] + [
        lax.ppermute(send[k], "x", [(i, (i + k) % nx) for i in range(nx)]) for k in range(1, nx)
    ]
    arrived = jnp.concatenate(arrived, axis=0)
    rows = lax.all_gather(arrived, ("c", "y", "z"), axis=0, tiled=True)
    gate_up_weight = jnp.concatenate([gate_weight, up_weight], axis=1)
    line_rows = rows.shape[0] // nc
    other_rows = lax.dynamic_slice_in_dim(rows, (1 - ci) * line_rows, line_rows, 0)
    own_rows = lax.dynamic_slice_in_dim(rows, ci * line_rows, line_rows, 0)
    other_out = expert_rows(other_rows, gate_up_weight, down_weight)
    other_back = lax.ppermute(other_out, "c", core_swap)
    own_out = expert_rows(own_rows, gate_up_weight, down_weight)
    summed = (own_out.astype(jnp.float32) + other_back.astype(jnp.float32)).astype(jnp.bfloat16)

    lines = summed.reshape(-1, experts * capacity, model_width)
    summed = jnp.sum(
        lax.all_to_all(lines, ("y", "z"), split_axis=0, concat_axis=0, tiled=True).astype(
            jnp.float32
        ),
        axis=0,
    )
    summed = summed.reshape(experts, capacity, model_width).astype(jnp.bfloat16)
    returned = jnp.stack(
        [summed[0]]
        + [
            lax.ppermute(summed[k], "x", [(i, (i - k) % nx) for i in range(nx)])
            for k in range(1, nx)
        ]
    )

    weights = jnp.where(hits, gate_cols[:, :, None], 0.0)
    moe = jnp.einsum(
        "rec,ecd->rd", weights, returned.astype(jnp.float32), precision=lax.Precision.HIGHEST
    )
    return (hidden_state + moe).astype(jnp.bfloat16)


def solution(mesh):
    dp_size = mesh.shape["dp"]

    def run(*args):
        experts = args[6].shape[1]
        ex_size = mesh.shape["expert"]
        devices = np.asarray(mesh.devices).reshape(
            dp_size // CORES, CORES, experts, ex_size // experts
        )
        fine = Mesh(devices, ("z", "c", "x", "y"))
        tok = ("z", "c")
        grp = ("x", "y")
        placed = (
            P(tok, None),
            P(None, grp),
            P(None, grp),
            P(grp, None),
            P(),
            P(tok + grp, None),
            P(),
            P(None, grp + tok),
            P(None, grp + tok),
            P(grp + tok, None),
        )
        body = jax.shard_map(
            per_device, mesh=fine, in_specs=placed, out_specs=P(tok + grp, None), check_vma=False
        )
        return body(*args)

    return run
```
